512 devices in a mesh: particle: 32 (over x, z), band: 16 (over y, core).
Axes of the slice: x: 4, y: 8, z: 8, core: 2. Of those that a mesh axis runs over, the one named last changes fastest.
Arguments:
- states: float32 [128, 2, 256, 1024], P('particle', None, 'band'), may hold values from -4 to 4
- counts: int32 [128], replicated, may hold values from 0 to 2, as said below
Outputs:
- forecast: float32 [128, 2, 256, 1024], P('particle', None, 'band')
The draws below stay inside these ranges and needn't reach their ends.
Inputs may be any that keep to these rules, and one draw needn't show every extreme that they name: Counts sum to 128; particle 0 and particle 128 - 1 have count 1, and for every m the particles 2m + 1 and 2m + 2 have counts summing to 2, so each slot's ancestor is the slot itself or a particle next to it; where 2m + 2 is a multiple of 4, the pair's counts are (2, 0).
All inputs are finite; a program needn't handle non-finite values.
Results may differ from the reference program's by a relative error of at most 0.00002.
Values sent between devices are 32-bit elements; how exact they have to be, the bound alone decides.
No kernel may reach another device: no remote copies, remote signals or barrier semaphores. Data moves between devices by JAX's collectives and lax.ppermute only.
A program may use at most 64 MiB of HBM per device.

```python
import jax
import jax.numpy as jnp
from jax import lax

P_DEV = 4
NX = 1024
GRID_HIERARCHY = 3
COARSE_SWEEPS = 6
NP = 128
NY = 256


def draw_counts(key, part):
    pair_count = NP // 2 - 1
    first_particle = 2 * jnp.arange(pair_count, dtype=jnp.int32) + 2
    straddle = first_particle % P_DEV == 0
    unbound_layout = jax.random.randint(jax.random.fold_in(key, 11), (pair_count,), 0, 3)
    pattern = jnp.where(straddle, 1, unbound_layout)
    leading = jnp.where(pattern == 0, 1, jnp.where(pattern == 1, 2, 0)).astype(jnp.int32)
    trailing = (2 - leading).astype(jnp.int32)
    middle = jnp.stack([leading, trailing], axis=1).reshape(-1)
    single = jnp.ones((1,), jnp.int32)
    return jnp.concatenate([single, middle, single])


def draw_states(key, part):
    domain_span = (NP, 2, NY, NX)
    noise = jax.random.normal(jax.random.fold_in(key, 22), domain_span, jnp.float32)
    return jnp.clip(noise, -4.0, 4.0)


def setup_inputs(seed: int = 0) -> dict:
    arg_keys = jax.random.split(jax.random.key(seed), 3)
    states = draw_states(jax.random.fold_in(arg_keys[2], 71), 0)
    counts = draw_counts(jax.random.fold_in(arg_keys[2], 71), 0)
    return {"states": states, "counts": counts}


smoothing_weight = 0.8
deform_term = 0.1
beta_slope = 0.5
bottom_friction_coefficient = 0.2
time_step = 0.5
meridional_weight = 1.8
zonal_weight = 0.2


def zero_rows(field):
    border = jnp.zeros_like(field[..., :1, :])
    return jnp.concatenate([border, field, border], axis=-2)


def neighbours(field, widened_field):
    across = widened_field[..., 2:, :] + widened_field[..., :-2, :]
    along = jnp.roll(field, -1, axis=-1) + jnp.roll(field, 1, axis=-1)
    return meridional_weight * across + zonal_weight * along


def smooth(field, forcing_term, diagonal_term):
    applied = diagonal_term * field - neighbours(field, zero_rows(field))
    return field + smoothing_weight * (forcing_term - applied) / diagonal_term


def restrict(field):
    leading = field.shape[:-2]
    height, breadth = field.shape[-2], field.shape[-1]
    blocks = field.reshape(leading + (height // 2, 2, breadth // 2, 2))
    return jnp.sum(blocks, axis=(-3, -1))


def prolong(field):
    return jnp.repeat(jnp.repeat(field, 2, axis=-2), 2, axis=-1)


def diagonal_at(level):
    return 4.0 + jnp.array([0.0, deform_term], jnp.float32).reshape(2, 1, 1) * (4.0 ** level)


def cycle(forcing_term, level):
    diagonal_term = diagonal_at(level)
    field = smoothing_weight * forcing_term / diagonal_term
    if level == GRID_HIERARCHY - 1:
        for repeat in range(COARSE_SWEEPS - 1):
            field = smooth(field, forcing_term, diagonal_term)
        return field
    field = smooth(field, forcing_term, diagonal_term)
    remainder = forcing_term - (diagonal_term * field - neighbours(field, zero_rows(field)))
    field = field + prolong(cycle(restrict(remainder), level + 1))
    field = smooth(field, forcing_term, diagonal_term)
    field = smooth(field, forcing_term, diagonal_term)
    return field


def advance_step(potential_curl_grid, stream, padded_stream, padded_vorticity):
    stream_x = 0.5 * (jnp.roll(stream, -1, axis=-1) - jnp.roll(stream, 1, axis=-1))
    meridional_streamfunction_gradient = 0.5 * (padded_stream[..., 2:, :] - padded_stream[..., :-2, :])
    vort_x = 0.5 * (jnp.roll(potential_curl_grid, -1, axis=-1) - jnp.roll(potential_curl_grid, 1, axis=-1))
    vort_y = 0.5 * (padded_vorticity[..., 2:, :] - padded_vorticity[..., :-2, :])
    laplace = neighbours(stream, padded_stream) - 4.0 * stream
    drag = jnp.array([0.0, bottom_friction_coefficient], jnp.float32).reshape(2, 1, 1)
    jacobian = stream_x * vort_y - meridional_streamfunction_gradient * vort_x
    return potential_curl_grid - time_step * (jacobian + beta_slope * stream_x + drag * laplace)


def lone_prediction_update(potential_curl_grid):
    upper = potential_curl_grid[..., 0, :, :]
    lower = potential_curl_grid[..., 1, :, :]
    forcing_term = -jnp.stack([0.5 * (upper + lower), 0.5 * (upper - lower)], axis=-3)
    modes = cycle(forcing_term, 0)
    stream = jnp.stack([modes[..., 0, :, :] + modes[..., 1, :, :], modes[..., 0, :, :] - modes[..., 1, :, :]], axis=-3)
    return advance_step(potential_curl_grid, stream, zero_rows(stream), zero_rows(potential_curl_grid))


def reference(states, counts):
    totals = jnp.cumsum(counts, dtype=jnp.int32)
    slots = jnp.arange(NP, dtype=jnp.int32)
    ancestor = jnp.sum((totals[None, :] <= slots[:, None]).astype(jnp.int32), axis=1, dtype=jnp.int32)
    redrawn_ensemble = jnp.take(states, ancestor, axis=0)
    return lax.map(lone_prediction_update, redrawn_ensemble)
```

```python
import numpy as np
import jax
import jax.numpy as jnp
from jax import lax
from jax.experimental import pallas as pl
from jax.experimental.pallas import tpu as pltpu
from jax.sharding import PartitionSpec as P

GRID_HIERARCHY = 3
COARSE_SWEEPS = 6


smoothing_weight = 0.8
deform_term = 0.1
beta_slope = 0.5
bottom_friction_coefficient = 0.2
time_step = 0.5
meridional_weight = 1.8
zonal_weight = 0.2

SLOTS = 4
FIELDS = 2 * SLOTS
ROWS0 = 16
COLS0 = 1024
F0 = 3 * ROWS0
F1 = F0 // 2
F2 = F1
CHUNK = 8


def diag(level, mode):
    extra = np.float32(deform_term) * np.float32(4.0**level) if mode else np.float32(0.0)
    return float(np.float32(4.0) + extra)


def shifted(value, axis, steps):
    count = lax.axis_size(axis)
    first, last = (max(0, -steps), min(count, count - steps))
    return lax.ppermute(value, axis, [(source, source + steps) for source in range(first, last)])


def rolled(x, shift, axis):
    return pltpu.roll(x, shift % x.shape[axis], axis)


def stencil(f):
    up = rolled(f, -1, 0)
    down = rolled(f, 1, 0)
    along = rolled(f, -1, 1) + rolled(f, 1, 1)
    return meridional_weight * (up + down) + zonal_weight * along


def smooth(f, s, d, mask):
    applied = d * f - stencil(f)
    out = f + smoothing_weight * (s - applied) / d
    return jnp.where(mask, out, 0.0)


def residual(f, s, d, mask):
    return jnp.where(mask, s - (d * f - stencil(f)), 0.0)


def row_mask(band, count, lo, per_device, total):
    rows = band * per_device + lo + lax.broadcasted_iota(jnp.int32, (count, 1), 0)
    return (rows >= 0) & (rows < total)


def pair_matrix(fine, coarse_first):
    if coarse_first:
        shape, fine_dim = (fine // 2, fine), 1
    else:
        shape, fine_dim = (fine, fine // 2), 0
    f_idx = lax.broadcasted_iota(jnp.int32, shape, fine_dim)
    c_idx = lax.broadcasted_iota(jnp.int32, shape, 1 - fine_dim)
    return jnp.where(jnp.right_shift(f_idx, 1) == c_idx, 1.0, 0.0).astype(jnp.bfloat16)


def split_dot(x, m):
    hi = x.astype(jnp.bfloat16)
    rest = x - hi.astype(jnp.float32)
    mid = rest.astype(jnp.bfloat16)
    lo = (rest - mid.astype(jnp.float32)).astype(jnp.bfloat16)
    out = jnp.dot(hi, m, preferred_element_type=jnp.float32)
    out = out + jnp.dot(mid, m, preferred_element_type=jnp.float32)
    return out + jnp.dot(lo, m, preferred_element_type=jnp.float32)


def put_blocks(ref, rows, value):
    for j in range(ref.shape[0]):
        ref[j, rows, :] = value[:, j * 128 : (j + 1) * 128]


def get_blocks(ref, rows):
    return jnp.concatenate([ref[j, rows, :] for j in range(ref.shape[0])], axis=1)


def sources(lo_ref, own_ref, hi_ref, slot):
    q = [
        jnp.concatenate([lo_ref[slot, layer], own_ref[slot, layer], hi_ref[slot, layer]], axis=0)
        for layer in range(2)
    ]
    return q, [-(0.5 * (q[0] + q[1])), -(0.5 * (q[0] - q[1]))]


def first_kernel(band_ref, lo_ref, own_ref, hi_ref, f1_ref, s1_ref, g1_ref, t_ref, r0_ref, r1_ref):
    band = band_ref[0]
    mask0 = row_mask(band, F0, -ROWS0, ROWS0, ROWS0 * 16)
    for slot in range(SLOTS):
        _, src = sources(lo_ref, own_ref, hi_ref, slot)
        for mode in range(2):
            d = diag(0, mode)
            s = src[mode]
            f0 = smoothing_weight * s / d
            f1 = smooth(f0, s, d, mask0)
            rows = pl.ds((2 * slot + mode) * F0, F0)
            f1_ref[rows, :] = f1
            put_blocks(r0_ref, rows, residual(f1, s, d, mask0))
    half = FIELDS * F1
    paired = get_blocks(r0_ref, pl.ds(0, half, stride=2)) + get_blocks(r0_ref, pl.ds(1, half, stride=2))
    s1_ref[...] = split_dot(paired, pair_matrix(COLS0, False))
    mask1 = row_mask(band, F1, -ROWS0 // 2, ROWS0 // 2, ROWS0 * 8)
    for field in range(FIELDS):
        d = diag(1, field % 2)
        rows = pl.ds(field * F1, F1)
        s = s1_ref[rows, :]
        g0 = smoothing_weight * s / d
        g1 = smooth(g0, s, d, mask1)
        g1_ref[rows, :] = g1
        put_blocks(r1_ref, rows, residual(g1, s, d, mask1))
    chunks = []
    for field in range(FIELDS):
        start = field * F1 + ROWS0 // 2
        chunks.append(
            get_blocks(r1_ref, pl.ds(start, CHUNK, stride=2))
            + get_blocks(r1_ref, pl.ds(start + 1, CHUNK, stride=2))
        )
    paired = jnp.concatenate(chunks, axis=0)
    keep = jnp.bitwise_and(lax.broadcasted_iota(jnp.int32, (FIELDS * CHUNK, 1), 0), CHUNK - 1) < ROWS0 // 4
    paired = jnp.where(keep, paired, 0.0)
    t_ref[...] = split_dot(paired, pair_matrix(COLS0 // 2, False))


def second_kernel(
    band_ref, lo_ref, own_ref, hi_ref, f1_ref, s1_ref, g1_ref,
    tm2_ref, tm1_ref, t0_ref, tp1_ref, tp2_ref,
    out_ref,
    s2_ref, e2_ref, up1_ref, g4_ref, up0_ref,
):
    band = band_ref[0]
    below = rolled(tm1_ref[...], CHUNK // 2, 0)
    above = rolled(tp1_ref[...], CHUNK // 2, 0)
    for field in range(FIELDS):
        piece = pl.ds(field * CHUNK, CHUNK)
        base = field * F2
        s2_ref[pl.ds(base, CHUNK), :] = tm2_ref[piece, :] + below[field * CHUNK : (field + 1) * CHUNK]
        s2_ref[pl.ds(base + CHUNK, CHUNK), :] = t0_ref[piece, :] + above[field * CHUNK : (field + 1) * CHUNK]
        s2_ref[pl.ds(base + 2 * CHUNK, CHUNK), :] = tp2_ref[piece, :]
    mask2 = row_mask(band, F2, -CHUNK, ROWS0 // 4, ROWS0 * 4)
    for field in range(FIELDS):
        d = diag(2, field % 2)
        rows = pl.ds(field * F2, F2)
        s = s2_ref[rows, :]
        e = smoothing_weight * s / d
        for repeat in range(COARSE_SWEEPS - 1):
            e = smooth(e, s, d, mask2)
        e2_ref[rows, :] = e
    cols = split_dot(e2_ref[...], pair_matrix(COLS0 // 2, True))
    n2 = FIELDS * F2
    put_blocks(up1_ref, pl.ds(0, n2, stride=2), cols)
    put_blocks(up1_ref, pl.ds(1, n2, stride=2), cols)
    mask1 = row_mask(band, F1, -ROWS0 // 2, ROWS0 // 2, ROWS0 * 8)
    for field in range(FIELDS):
        d = diag(1, field % 2)
        rows = pl.ds(field * F1, F1)
        s = s1_ref[rows, :]
        g2 = g1_ref[rows, :] + get_blocks(up1_ref, pl.ds(field * 2 * F2 + CHUNK, F1))
        g3 = smooth(g2, s, d, mask1)
        g4_ref[rows, :] = smooth(g3, s, d, mask1)
    cols = split_dot(g4_ref[...], pair_matrix(COLS0, True))
    n1 = FIELDS * F1
    put_blocks(up0_ref, pl.ds(0, n1, stride=2), cols)
    put_blocks(up0_ref, pl.ds(1, n1, stride=2), cols)
    mask0 = row_mask(band, F0, -ROWS0, ROWS0, ROWS0 * 16)
    for slot in range(SLOTS):
        q, src = sources(lo_ref, own_ref, hi_ref, slot)
        modes = []
        for mode in range(2):
            d = diag(0, mode)
            rows = pl.ds((2 * slot + mode) * F0, F0)
            f2 = f1_ref[rows, :] + get_blocks(up0_ref, rows)
            f3 = smooth(f2, src[mode], d, mask0)
            modes.append(smooth(f3, src[mode], d, mask0))
        streams = [modes[0] + modes[1], modes[0] - modes[1]]
        for layer in range(2):
            stream = streams[layer]
            pv = q[layer]
            stream_x = 0.5 * (rolled(stream, -1, 1) - rolled(stream, 1, 1))
            stream_y = 0.5 * (rolled(stream, -1, 0) - rolled(stream, 1, 0))
            vort_x = 0.5 * (rolled(pv, -1, 1) - rolled(pv, 1, 1))
            vort_y = 0.5 * (rolled(pv, -1, 0) - rolled(pv, 1, 0))
            laplace = stencil(stream) - 4.0 * stream
            drag = bottom_friction_coefficient if layer else 0.0
            jacobian = stream_x * vort_y - stream_y * vort_x
            new = pv - time_step * (jacobian + beta_slope * stream_x + drag * laplace)
            out_ref[slot, layer] = new[ROWS0 : 2 * ROWS0]


def vmem():
    return pl.BlockSpec(memory_space=pltpu.VMEM)


def smem():
    return pl.BlockSpec(memory_space=pltpu.SMEM)


PARAMS = pltpu.CompilerParams(vmem_limit_bytes=48 * 1024 * 1024)


def per_device(states, counts):
    group = lax.axis_index("particle")
    per_group = states.shape[0]
    totals = jnp.cumsum(counts, dtype=jnp.int32)
    slots = group * per_group + jnp.arange(per_group, dtype=jnp.int32)
    ancestor = jnp.sum(
        (totals[None, :] <= slots[:, None]).astype(jnp.int32), axis=1, dtype=jnp.int32
    )
    below_last = shifted(states[-1:], "particle", 1)
    extended = jnp.concatenate([below_last, states], axis=0)
    local_index = ancestor - (group * per_group - 1)
    redrawn = jnp.take(extended, local_index, axis=0)

    band = lax.axis_index("band").astype(jnp.int32).reshape(1)
    lo_q = shifted(redrawn, "band", 1)
    hi_q = shifted(redrawn, "band", -1)
    f32 = jnp.float32
    f1, s1, g1, t = pl.pallas_call(
        first_kernel,
        out_shape=(
            jax.ShapeDtypeStruct((FIELDS * F0, COLS0), f32),
            jax.ShapeDtypeStruct((FIELDS * F1, COLS0 // 2), f32),
            jax.ShapeDtypeStruct((FIELDS * F1, COLS0 // 2), f32),
            jax.ShapeDtypeStruct((FIELDS * CHUNK, COLS0 // 4), f32),
        ),
        in_specs=[smem(), vmem(), vmem(), vmem()],
        out_specs=(vmem(), vmem(), vmem(), vmem()),
        scratch_shapes=[
            pltpu.VMEM((COLS0 // 128, FIELDS * F0, 128), f32),
            pltpu.VMEM((COLS0 // 256, FIELDS * F1, 128), f32),
        ],
        compiler_params=PARAMS,
    )(band, lo_q, redrawn, hi_q)
    tm2 = shifted(t, "band", 2)
    tm1 = shifted(t, "band", 1)
    tp1 = shifted(t, "band", -1)
    tp2 = shifted(t, "band", -2)
    return pl.pallas_call(
        second_kernel,
        out_shape=jax.ShapeDtypeStruct(redrawn.shape, f32),
        in_specs=[smem()] + [vmem()] * 11,
        out_specs=vmem(),
        scratch_shapes=[
            pltpu.VMEM((FIELDS * F2, COLS0 // 4), f32),
            pltpu.VMEM((FIELDS * F2, COLS0 // 4), f32),
            pltpu.VMEM((COLS0 // 256, 2 * FIELDS * F2, 128), f32),
            pltpu.VMEM((FIELDS * F1, COLS0 // 2), f32),
            pltpu.VMEM((COLS0 // 128, FIELDS * F0, 128), f32),
        ],
        compiler_params=PARAMS,
    )(band, lo_q, redrawn, hi_q, f1, s1, g1, tm2, tm1, t, tp1, tp2)


def solution(mesh):
    in_specs = (P("particle", None, "band", None), P())
    out_specs = P("particle", None, "band", None)
    return jax.shard_map(
        per_device, mesh=mesh, in_specs=in_specs, out_specs=out_specs, check_vma=False
    )
```

```python
import functools

import numpy as np
import jax
import jax.numpy as jnp
from jax import lax
from jax.experimental import pallas as pl
from jax.experimental.pallas import tpu as pltpu
from jax.sharding import PartitionSpec as P

GRID_HIERARCHY = 3
COARSE_SWEEPS = 6


smoothing_weight = 0.8
deform_term = 0.1
beta_slope = 0.5
bottom_friction_coefficient = 0.2
time_step = 0.5
meridional_weight = 1.8
zonal_weight = 0.2

SLOTS = 4
FIELDS = 2 * SLOTS
ROWS0 = 16
COLS0 = 1024
F0 = 3 * ROWS0
F1 = F0 // 2
F2 = F1
CHUNK = 8


def diag(level, mode):
    extra = np.float32(deform_term) * np.float32(4.0**level) if mode else np.float32(0.0)
    return float(np.float32(4.0) + extra)


def shifted(value, axis, steps):
    count = lax.axis_size(axis)
    first, last = (max(0, -steps), min(count, count - steps))
    return lax.ppermute(value, axis, [(source, source + steps) for source in range(first, last)])


def rolled(x, shift, axis):
    return pltpu.roll(x, shift % x.shape[axis], axis)


def stencil(f):
    up = rolled(f, -1, 0)
    down = rolled(f, 1, 0)
    along = rolled(f, -1, 1) + rolled(f, 1, 1)
    return meridional_weight * (up + down) + zonal_weight * along


def smooth(f, s, d, mask):
    applied = d * f - stencil(f)
    out = f + smoothing_weight * (s - applied) / d
    return jnp.where(mask, out, 0.0)


def residual(f, s, d, mask):
    return jnp.where(mask, s - (d * f - stencil(f)), 0.0)


def row_mask(band, count, lo, per_device, total):
    rows = band * per_device + lo + lax.broadcasted_iota(jnp.int32, (count, 1), 0)
    return (rows >= 0) & (rows < total)


def pair_matrix(fine, coarse_first):
    if coarse_first:
        shape, fine_dim = (fine // 2, fine), 1
    else:
        shape, fine_dim = (fine, fine // 2), 0
    f_idx = lax.broadcasted_iota(jnp.int32, shape, fine_dim)
    c_idx = lax.broadcasted_iota(jnp.int32, shape, 1 - fine_dim)
    return jnp.where(jnp.right_shift(f_idx, 1) == c_idx, 1.0, 0.0).astype(jnp.bfloat16)


def split_dot(x, m):
    hi = x.astype(jnp.bfloat16)
    rest = x - hi.astype(jnp.float32)
    mid = rest.astype(jnp.bfloat16)
    lo = (rest - mid.astype(jnp.float32)).astype(jnp.bfloat16)
    out = jnp.dot(hi, m, preferred_element_type=jnp.float32)
    out = out + jnp.dot(mid, m, preferred_element_type=jnp.float32)
    return out + jnp.dot(lo, m, preferred_element_type=jnp.float32)


def put_blocks(ref, rows, value):
    for j in range(ref.shape[0]):
        ref[j, rows, :] = value[:, j * 128 : (j + 1) * 128]


def get_blocks(ref, rows):
    return jnp.concatenate([ref[j, rows, :] for j in range(ref.shape[0])], axis=1)


def sources(lo_ref, own_ref, hi_ref, slot):
    q = [
        jnp.concatenate([lo_ref[slot, layer], own_ref[slot, layer], hi_ref[slot, layer]], axis=0)
        for layer in range(2)
    ]
    return q, [-(0.5 * (q[0] + q[1])), -(0.5 * (q[0] - q[1]))]


def first_kernel(band_ref, lo_ref, own_ref, hi_ref, f1_ref, s1_ref, g1_ref, t_ref, r0_ref, r1_ref):
    band = band_ref[0]
    mask0 = row_mask(band, F0, -ROWS0, ROWS0, ROWS0 * 16)
    for slot in range(SLOTS):
        _, src = sources(lo_ref, own_ref, hi_ref, slot)
        for mode in range(2):
            d = diag(0, mode)
            s = src[mode]
            f0 = smoothing_weight * s / d
            f1 = smooth(f0, s, d, mask0)
            rows = pl.ds((2 * slot + mode) * F0, F0)
            f1_ref[rows, :] = f1
            put_blocks(r0_ref, rows, residual(f1, s, d, mask0))
    half = FIELDS * F1
    paired = get_blocks(r0_ref, pl.ds(0, half, stride=2)) + get_blocks(r0_ref, pl.ds(1, half, stride=2))
    s1_ref[...] = split_dot(paired, pair_matrix(COLS0, False))
    mask1 = row_mask(band, F1, -ROWS0 // 2, ROWS0 // 2, ROWS0 * 8)
    for field in range(FIELDS):
        d = diag(1, field % 2)
        rows = pl.ds(field * F1, F1)
        s = s1_ref[rows, :]
        g0 = smoothing_weight * s / d
        g1 = smooth(g0, s, d, mask1)
        g1_ref[rows, :] = g1
        put_blocks(r1_ref, rows, residual(g1, s, d, mask1))
    chunks = []
    for field in range(FIELDS):
        start = field * F1 + ROWS0 // 2
        chunks.append(
            get_blocks(r1_ref, pl.ds(start, CHUNK, stride=2))
            + get_blocks(r1_ref, pl.ds(start + 1, CHUNK, stride=2))
        )
    paired = jnp.concatenate(chunks, axis=0)
    keep = jnp.bitwise_and(lax.broadcasted_iota(jnp.int32, (FIELDS * CHUNK, 1), 0), CHUNK - 1) < ROWS0 // 4
    paired = jnp.where(keep, paired, 0.0)
    t_ref[...] = split_dot(paired, pair_matrix(COLS0 // 2, False))


def second_kernel(
    slots, band_ref, lo_ref, own_ref, hi_ref, f1_ref, s1_ref, g1_ref,
    tm2_ref, tm1_ref, t0_ref, tp1_ref, tp2_ref,
    out_ref,
    s2_ref, e2_ref, up1_ref, g4_ref, up0_ref,
):
    fields = 2 * slots
    band = band_ref[0]
    below = rolled(tm1_ref[...], CHUNK // 2, 0)
    above = rolled(tp1_ref[...], CHUNK // 2, 0)
    for field in range(fields):
        piece = pl.ds(field * CHUNK, CHUNK)
        base = field * F2
        s2_ref[pl.ds(base, CHUNK), :] = tm2_ref[piece, :] + below[field * CHUNK : (field + 1) * CHUNK]
        s2_ref[pl.ds(base + CHUNK, CHUNK), :] = t0_ref[piece, :] + above[field * CHUNK : (field + 1) * CHUNK]
        s2_ref[pl.ds(base + 2 * CHUNK, CHUNK), :] = tp2_ref[piece, :]
    mask2 = row_mask(band, F2, -CHUNK, ROWS0 // 4, ROWS0 * 4)
    for field in range(fields):
        d = diag(2, field % 2)
        rows = pl.ds(field * F2, F2)
        s = s2_ref[rows, :]
        e = smoothing_weight * s / d
        for repeat in range(COARSE_SWEEPS - 1):
            e = smooth(e, s, d, mask2)
        e2_ref[rows, :] = e
    cols = split_dot(e2_ref[...], pair_matrix(COLS0 // 2, True))
    n2 = fields * F2
    put_blocks(up1_ref, pl.ds(0, n2, stride=2), cols)
    put_blocks(up1_ref, pl.ds(1, n2, stride=2), cols)
    mask1 = row_mask(band, F1, -ROWS0 // 2, ROWS0 // 2, ROWS0 * 8)
    for field in range(fields):
        d = diag(1, field % 2)
        rows = pl.ds(field * F1, F1)
        s = s1_ref[rows, :]
        g2 = g1_ref[rows, :] + get_blocks(up1_ref, pl.ds(field * 2 * F2 + CHUNK, F1))
        g3 = smooth(g2, s, d, mask1)
        g4_ref[rows, :] = smooth(g3, s, d, mask1)
    cols = split_dot(g4_ref[...], pair_matrix(COLS0, True))
    n1 = fields * F1
    put_blocks(up0_ref, pl.ds(0, n1, stride=2), cols)
    put_blocks(up0_ref, pl.ds(1, n1, stride=2), cols)
    mask0 = row_mask(band, F0, -ROWS0, ROWS0, ROWS0 * 16)
    for slot in range(slots):
        q, src = sources(lo_ref, own_ref, hi_ref, slot)
        modes = []
        for mode in range(2):
            d = diag(0, mode)
            rows = pl.ds((2 * slot + mode) * F0, F0)
            f2 = f1_ref[rows, :] + get_blocks(up0_ref, rows)
            f3 = smooth(f2, src[mode], d, mask0)
            modes.append(smooth(f3, src[mode], d, mask0))
        streams = [modes[0] + modes[1], modes[0] - modes[1]]
        for layer in range(2):
            stream = streams[layer]
            pv = q[layer]
            stream_x = 0.5 * (rolled(stream, -1, 1) - rolled(stream, 1, 1))
            stream_y = 0.5 * (rolled(stream, -1, 0) - rolled(stream, 1, 0))
            vort_x = 0.5 * (rolled(pv, -1, 1) - rolled(pv, 1, 1))
            vort_y = 0.5 * (rolled(pv, -1, 0) - rolled(pv, 1, 0))
            laplace = stencil(stream) - 4.0 * stream
            drag = bottom_friction_coefficient if layer else 0.0
            jacobian = stream_x * vort_y - stream_y * vort_x
            new = pv - time_step * (jacobian + beta_slope * stream_x + drag * laplace)
            out_ref[slot, layer] = new[ROWS0 : 2 * ROWS0]


def pick_kernel(index_ref, below_ref, last_ref, rest_ref, out_ref):
    for slot in range(SLOTS):
        index = index_ref[slot]
        value = last_ref[0]
        for k in range(SLOTS - 2, -1, -1):
            value = jnp.where(index == k + 1, rest_ref[k], value)
        out_ref[slot] = jnp.where(index == 0, below_ref[0], value)


def vmem():
    return pl.BlockSpec(memory_space=pltpu.VMEM)


def smem():
    return pl.BlockSpec(memory_space=pltpu.SMEM)


PARAMS = pltpu.CompilerParams(vmem_limit_bytes=48 * 1024 * 1024)


def per_device(states, counts):
    group = lax.axis_index("particle")
    per_group = states.shape[0]
    totals = jnp.cumsum(counts, dtype=jnp.int32)
    slots = group * per_group + jnp.arange(per_group, dtype=jnp.int32)
    ancestor = jnp.sum(
        (totals[None, :] <= slots[:, None]).astype(jnp.int32), axis=1, dtype=jnp.int32
    )
    local_index = ancestor - (group * per_group - 1)

    band = lax.axis_index("band").astype(jnp.int32).reshape(1)
    lo_q = shifted(states, "band", 1)
    hi_q = shifted(states, "band", -1)
    f32 = jnp.float32
    f1, s1, g1, t = pl.pallas_call(
        first_kernel,
        out_shape=(
            jax.ShapeDtypeStruct((FIELDS * F0, COLS0), f32),
            jax.ShapeDtypeStruct((FIELDS * F1, COLS0 // 2), f32),
            jax.ShapeDtypeStruct((FIELDS * F1, COLS0 // 2), f32),
            jax.ShapeDtypeStruct((FIELDS * CHUNK, COLS0 // 4), f32),
        ),
        in_specs=[smem(), vmem(), vmem(), vmem()],
        out_specs=(vmem(), vmem(), vmem(), vmem()),
        scratch_shapes=[
            pltpu.VMEM((COLS0 // 128, FIELDS * F0, 128), f32),
            pltpu.VMEM((COLS0 // 256, FIELDS * F1, 128), f32),
        ],
        compiler_params=PARAMS,
    )(band, lo_q, states, hi_q)
    tm2 = shifted(t, "band", 2)
    tm1 = shifted(t, "band", 1)
    tp1 = shifted(t, "band", -1)
    tp2 = shifted(t, "band", -2)
    args = (band, lo_q, states, hi_q, f1, s1, g1, tm2, tm1, t, tp1, tp2)
    last = forecast_slots(SLOTS - 1, 1, args)
    below = shifted(last, "particle", 1)
    rest = forecast_slots(0, SLOTS - 1, args)
    return pl.pallas_call(
        pick_kernel,
        out_shape=jax.ShapeDtypeStruct(states.shape, f32),
        in_specs=[smem(), vmem(), vmem(), vmem()],
        out_specs=vmem(),
    )(local_index, below, last, rest)


def forecast_slots(first, slots, args):
    fields = 2 * slots
    block = first // slots

    def rows(count, width):
        return pl.BlockSpec((count, width), lambda i: (block, 0))

    strips = pl.BlockSpec((slots, 2, ROWS0, COLS0), lambda i: (block, 0, 0, 0))
    in_specs = [smem(), strips, strips, strips,
                rows(fields * F0, COLS0), rows(fields * F1, COLS0 // 2), rows(fields * F1, COLS0 // 2)]
    in_specs += [rows(fields * CHUNK, COLS0 // 4)] * 5
    f32 = jnp.float32
    work = fields * F0 * COLS0 * 160
    return pl.pallas_call(
        functools.partial(second_kernel, slots),
        out_shape=jax.ShapeDtypeStruct((slots, 2, ROWS0, COLS0), f32),
        grid=(1,),
        in_specs=in_specs,
        out_specs=pl.BlockSpec((slots, 2, ROWS0, COLS0), lambda i: (0, 0, 0, 0)),
        scratch_shapes=[
            pltpu.VMEM((fields * F2, COLS0 // 4), f32),
            pltpu.VMEM((fields * F2, COLS0 // 4), f32),
            pltpu.VMEM((COLS0 // 256, 2 * fields * F2, 128), f32),
            pltpu.VMEM((fields * F1, COLS0 // 2), f32),
            pltpu.VMEM((COLS0 // 128, fields * F0, 128), f32),
        ],
        compiler_params=PARAMS,
        cost_estimate=pl.CostEstimate(flops=work, transcendentals=0, bytes_accessed=fields * F0 * COLS0 * 16),
    )(*args)


def solution(mesh):
    in_specs = (P("particle", None, "band", None), P())
    out_specs = P("particle", None, "band", None)
    return jax.shard_map(
        per_device, mesh=mesh, in_specs=in_specs, out_specs=out_specs, check_vma=False
    )
```

```python
import functools

import numpy as np
import jax
import jax.numpy as jnp
from jax import lax
from jax.experimental import pallas as pl
from jax.experimental.pallas import tpu as pltpu
from jax.sharding import PartitionSpec as P

GRID_HIERARCHY = 3
COARSE_SWEEPS = 6


smoothing_weight = 0.8
deform_term = 0.1
beta_slope = 0.5
bottom_friction_coefficient = 0.2
time_step = 0.5
meridional_weight = 1.8
zonal_weight = 0.2

SLOTS = 4
FIELDS = 2 * SLOTS
ROWS0 = 16
COLS0 = 1024
F0 = 3 * ROWS0
F1 = F0 // 2
F2 = F1
CHUNK = 8


def diag(level, mode):
    extra = np.float32(deform_term) * np.float32(4.0**level) if mode else np.float32(0.0)
    return float(np.float32(4.0) + extra)


def shifted(value, axis, steps):
    count = lax.axis_size(axis)
    first, last = (max(0, -steps), min(count, count - steps))
    return lax.ppermute(value, axis, [(source, source + steps) for source in range(first, last)])


def rolled(x, shift, axis):
    return pltpu.roll(x, shift % x.shape[axis], axis)


def stencil(f):
    up = rolled(f, -1, 0)
    down = rolled(f, 1, 0)
    along = rolled(f, -1, 1) + rolled(f, 1, 1)
    return meridional_weight * (up + down) + zonal_weight * along


def smooth(f, s, d, mask):
    applied = d * f - stencil(f)
    out = f + smoothing_weight * (s - applied) / d
    return jnp.where(mask, out, 0.0)


def residual(f, s, d, mask):
    return jnp.where(mask, s - (d * f - stencil(f)), 0.0)


def row_mask(band, count, lo, per_device, total):
    rows = band * per_device + lo + lax.broadcasted_iota(jnp.int32, (count, 1), 0)
    return (rows >= 0) & (rows < total)


def pair_matrix(fine, coarse_first):
    if coarse_first:
        shape, fine_dim = (fine // 2, fine), 1
    else:
        shape, fine_dim = (fine, fine // 2), 0
    f_idx = lax.broadcasted_iota(jnp.int32, shape, fine_dim)
    c_idx = lax.broadcasted_iota(jnp.int32, shape, 1 - fine_dim)
    return jnp.where(jnp.right_shift(f_idx, 1) == c_idx, 1.0, 0.0).astype(jnp.bfloat16)


def split_dot(x, m):
    hi = x.astype(jnp.bfloat16)
    rest = x - hi.astype(jnp.float32)
    mid = rest.astype(jnp.bfloat16)
    lo = (rest - mid.astype(jnp.float32)).astype(jnp.bfloat16)
    out = jnp.dot(hi, m, preferred_element_type=jnp.float32)
    out = out + jnp.dot(mid, m, preferred_element_type=jnp.float32)
    return out + jnp.dot(lo, m, preferred_element_type=jnp.float32)


def put_blocks(ref, rows, value):
    for j in range(ref.shape[0]):
        ref[j, rows, :] = value[:, j * 128 : (j + 1) * 128]


def get_blocks(ref, rows):
    return jnp.concatenate([ref[j, rows, :] for j in range(ref.shape[0])], axis=1)


def sources(refs, index_ref, slot):
    lo_ref, own_ref, hi_ref, blo_ref, bown_ref, bhi_ref = refs
    index = index_ref[slot]
    local = jnp.maximum(index - 1, 0)
    below = index == 0
    q = []
    for layer in range(2):
        pieces = [
            jnp.where(below, b_ref[0, layer], x_ref[local, layer])
            for b_ref, x_ref in ((blo_ref, lo_ref), (bown_ref, own_ref), (bhi_ref, hi_ref))
        ]
        q.append(jnp.concatenate(pieces, axis=0))
    return q, [-(0.5 * (q[0] + q[1])), -(0.5 * (q[0] - q[1]))]


def first_kernel(band_ref, index_ref, lo_ref, own_ref, hi_ref, blo_ref, bown_ref, bhi_ref, f1_ref, s1_ref, g1_ref, t_ref, r0_ref, r1_ref):
    band = band_ref[0]
    mask0 = row_mask(band, F0, -ROWS0, ROWS0, ROWS0 * 16)
    for slot in range(SLOTS):
        _, src = sources((lo_ref, own_ref, hi_ref, blo_ref, bown_ref, bhi_ref), index_ref, slot)
        for mode in range(2):
            d = diag(0, mode)
            s = src[mode]
            f0 = smoothing_weight * s / d
            f1 = smooth(f0, s, d, mask0)
            rows = pl.ds((2 * slot + mode) * F0, F0)
            f1_ref[rows, :] = f1
            put_blocks(r0_ref, rows, residual(f1, s, d, mask0))
    half = FIELDS * F1
    paired = get_blocks(r0_ref, pl.ds(0, half, stride=2)) + get_blocks(r0_ref, pl.ds(1, half, stride=2))
    s1_ref[...] = split_dot(paired, pair_matrix(COLS0, False))
    mask1 = row_mask(band, F1, -ROWS0 // 2, ROWS0 // 2, ROWS0 * 8)
    for field in range(FIELDS):
        d = diag(1, field % 2)
        rows = pl.ds(field * F1, F1)
        s = s1_ref[rows, :]
        g0 = smoothing_weight * s / d
        g1 = smooth(g0, s, d, mask1)
        g1_ref[rows, :] = g1
        put_blocks(r1_ref, rows, residual(g1, s, d, mask1))
    chunks = []
    for field in range(FIELDS):
        start = field * F1 + ROWS0 // 2
        chunks.append(
            get_blocks(r1_ref, pl.ds(start, CHUNK, stride=2))
            + get_blocks(r1_ref, pl.ds(start + 1, CHUNK, stride=2))
        )
    paired = jnp.concatenate(chunks, axis=0)
    keep = jnp.bitwise_and(lax.broadcasted_iota(jnp.int32, (FIELDS * CHUNK, 1), 0), CHUNK - 1) < ROWS0 // 4
    paired = jnp.where(keep, paired, 0.0)
    t_ref[...] = split_dot(paired, pair_matrix(COLS0 // 2, False))


def second_kernel(
    slots, band_ref, index_ref, lo_ref, own_ref, hi_ref, blo_ref, bown_ref, bhi_ref,
    f1_ref, s1_ref, g1_ref,
    tm2_ref, tm1_ref, t0_ref, tp1_ref, tp2_ref,
    out_ref,
    s2_ref, e2_ref, up1_ref, g4_ref, up0_ref,
):
    fields = 2 * slots
    band = band_ref[0]
    below = rolled(tm1_ref[...], CHUNK // 2, 0)
    above = rolled(tp1_ref[...], CHUNK // 2, 0)
    for field in range(fields):
        piece = pl.ds(field * CHUNK, CHUNK)
        base = field * F2
        s2_ref[pl.ds(base, CHUNK), :] = tm2_ref[piece, :] + below[field * CHUNK : (field + 1) * CHUNK]
        s2_ref[pl.ds(base + CHUNK, CHUNK), :] = t0_ref[piece, :] + above[field * CHUNK : (field + 1) * CHUNK]
        s2_ref[pl.ds(base + 2 * CHUNK, CHUNK), :] = tp2_ref[piece, :]
    mask2 = row_mask(band, F2, -CHUNK, ROWS0 // 4, ROWS0 * 4)
    for field in range(fields):
        d = diag(2, field % 2)
        rows = pl.ds(field * F2, F2)
        s = s2_ref[rows, :]
        e = smoothing_weight * s / d
        for repeat in range(COARSE_SWEEPS - 1):
            e = smooth(e, s, d, mask2)
        e2_ref[rows, :] = e
    cols = split_dot(e2_ref[...], pair_matrix(COLS0 // 2, True))
    n2 = fields * F2
    put_blocks(up1_ref, pl.ds(0, n2, stride=2), cols)
    put_blocks(up1_ref, pl.ds(1, n2, stride=2), cols)
    mask1 = row_mask(band, F1, -ROWS0 // 2, ROWS0 // 2, ROWS0 * 8)
    for field in range(fields):
        d = diag(1, field % 2)
        rows = pl.ds(field * F1, F1)
        s = s1_ref[rows, :]
        g2 = g1_ref[rows, :] + get_blocks(up1_ref, pl.ds(field * 2 * F2 + CHUNK, F1))
        g3 = smooth(g2, s, d, mask1)
        g4_ref[rows, :] = smooth(g3, s, d, mask1)
    cols = split_dot(g4_ref[...], pair_matrix(COLS0, True))
    n1 = fields * F1
    put_blocks(up0_ref, pl.ds(0, n1, stride=2), cols)
    put_blocks(up0_ref, pl.ds(1, n1, stride=2), cols)
    mask0 = row_mask(band, F0, -ROWS0, ROWS0, ROWS0 * 16)
    for slot in range(slots):
        q, src = sources((lo_ref, own_ref, hi_ref, blo_ref, bown_ref, bhi_ref), index_ref, slot)
        modes = []
        for mode in range(2):
            d = diag(0, mode)
            rows = pl.ds((2 * slot + mode) * F0, F0)
            f2 = f1_ref[rows, :] + get_blocks(up0_ref, rows)
            f3 = smooth(f2, src[mode], d, mask0)
            modes.append(smooth(f3, src[mode], d, mask0))
        streams = [modes[0] + modes[1], modes[0] - modes[1]]
        for layer in range(2):
            stream = streams[layer]
            pv = q[layer]
            stream_x = 0.5 * (rolled(stream, -1, 1) - rolled(stream, 1, 1))
            stream_y = 0.5 * (rolled(stream, -1, 0) - rolled(stream, 1, 0))
            vort_x = 0.5 * (rolled(pv, -1, 1) - rolled(pv, 1, 1))
            vort_y = 0.5 * (rolled(pv, -1, 0) - rolled(pv, 1, 0))
            laplace = stencil(stream) - 4.0 * stream
            drag = bottom_friction_coefficient if layer else 0.0
            jacobian = stream_x * vort_y - stream_y * vort_x
            new = pv - time_step * (jacobian + beta_slope * stream_x + drag * laplace)
            out_ref[slot, layer] = new[ROWS0 : 2 * ROWS0]


def vmem():
    return pl.BlockSpec(memory_space=pltpu.VMEM)


def smem():
    return pl.BlockSpec(memory_space=pltpu.SMEM)


PARAMS = pltpu.CompilerParams(vmem_limit_bytes=48 * 1024 * 1024)


def per_device(states, counts):
    group = lax.axis_index("particle")
    per_group = states.shape[0]
    totals = jnp.cumsum(counts, dtype=jnp.int32)
    slots = group * per_group + jnp.arange(per_group, dtype=jnp.int32)
    ancestor = jnp.sum(
        (totals[None, :] <= slots[:, None]).astype(jnp.int32), axis=1, dtype=jnp.int32
    )
    local_index = ancestor - (group * per_group - 1)

    band = lax.axis_index("band").astype(jnp.int32).reshape(1)
    lo_q = shifted(states, "band", 1)
    hi_q = shifted(states, "band", -1)
    last = states[per_group - 1 :]
    below_own = shifted(last, "particle", 1)
    below_lo = diagonal(last, 1, 1)
    below_hi = diagonal(last, 1, -1)
    pieces = (lo_q, states, hi_q, below_lo, below_own, below_hi)
    f32 = jnp.float32
    f1, s1, g1, t = pl.pallas_call(
        first_kernel,
        out_shape=(
            jax.ShapeDtypeStruct((FIELDS * F0, COLS0), f32),
            jax.ShapeDtypeStruct((FIELDS * F1, COLS0 // 2), f32),
            jax.ShapeDtypeStruct((FIELDS * F1, COLS0 // 2), f32),
            jax.ShapeDtypeStruct((FIELDS * CHUNK, COLS0 // 4), f32),
        ),
        in_specs=[smem(), smem()] + [vmem()] * 6,
        out_specs=(vmem(), vmem(), vmem(), vmem()),
        scratch_shapes=[
            pltpu.VMEM((COLS0 // 128, FIELDS * F0, 128), f32),
            pltpu.VMEM((COLS0 // 256, FIELDS * F1, 128), f32),
        ],
        compiler_params=PARAMS,
    )(band, local_index, *pieces)
    tm2 = shifted(t, "band", 2)
    tm1 = shifted(t, "band", 1)
    tp1 = shifted(t, "band", -1)
    tp2 = shifted(t, "band", -2)
    return forecast_slots(SLOTS, (band, local_index) + pieces + (f1, s1, g1, tm2, tm1, t, tp1, tp2))


def diagonal(value, particle_steps, band_steps):
    particles, bands = lax.axis_size("particle"), lax.axis_size("band")
    pairs = []
    for p in range(particles):
        for b in range(bands):
            tp, tb = p + particle_steps, b + band_steps
            if 0 <= tp < particles and 0 <= tb < bands:
                pairs.append((p * bands + b, tp * bands + tb))
    return lax.ppermute(value, ("particle", "band"), pairs)


def forecast_slots(slots, args):
    fields = 2 * slots
    f32 = jnp.float32
    work = fields * F0 * COLS0 * 160
    return pl.pallas_call(
        functools.partial(second_kernel, slots),
        out_shape=jax.ShapeDtypeStruct((slots, 2, ROWS0, COLS0), f32),
        in_specs=[smem(), smem()] + [vmem()] * (len(args) - 2),
        out_specs=vmem(),
        scratch_shapes=[
            pltpu.VMEM((fields * F2, COLS0 // 4), f32),
            pltpu.VMEM((fields * F2, COLS0 // 4), f32),
            pltpu.VMEM((COLS0 // 256, 2 * fields * F2, 128), f32),
            pltpu.VMEM((fields * F1, COLS0 // 2), f32),
            pltpu.VMEM((COLS0 // 128, fields * F0, 128), f32),
        ],
        compiler_params=PARAMS,
        cost_estimate=pl.CostEstimate(flops=work, transcendentals=0, bytes_accessed=fields * F0 * COLS0 * 16),
    )(*args)


def solution(mesh):
    in_specs = (P("particle", None, "band", None), P())
    out_specs = P("particle", None, "band", None)
    return jax.shard_map(
        per_device, mesh=mesh, in_specs=in_specs, out_specs=out_specs, check_vma=False
    )
```

```python
import functools

import numpy as np
import jax
import jax.numpy as jnp
from jax import lax
from jax.experimental import pallas as pl
from jax.experimental.pallas import tpu as pltpu
from jax.sharding import PartitionSpec as P

GRID_HIERARCHY = 3
COARSE_SWEEPS = 6


smoothing_weight = 0.8
deform_term = 0.1
beta_slope = 0.5
bottom_friction_coefficient = 0.2
time_step = 0.5
meridional_weight = 1.8
zonal_weight = 0.2

SLOTS = 4
FIELDS = 2 * SLOTS
ROWS0 = 16
COLS0 = 1024
F0 = 3 * ROWS0
F1 = F0 // 2
F2 = F1
CHUNK = 8


def diag(level, mode):
    extra = np.float32(deform_term) * np.float32(4.0**level) if mode else np.float32(0.0)
    return float(np.float32(4.0) + extra)


def shifted(value, axis, steps):
    count = lax.axis_size(axis)
    first, last = (max(0, -steps), min(count, count - steps))
    return lax.ppermute(value, axis, [(source, source + steps) for source in range(first, last)])


def rolled(x, shift, axis):
    return pltpu.roll(x, shift % x.shape[axis], axis)


def stencil(f):
    up = rolled(f, -1, 0)
    down = rolled(f, 1, 0)
    along = rolled(f, -1, 1) + rolled(f, 1, 1)
    return meridional_weight * (up + down) + zonal_weight * along


def smooth(f, s, d, mask):
    applied = d * f - stencil(f)
    out = f + smoothing_weight * (s - applied) / d
    return jnp.where(mask, out, 0.0)


def residual(f, s, d, mask):
    return jnp.where(mask, s - (d * f - stencil(f)), 0.0)


def row_mask(band, count, lo, per_device, total):
    rows = band * per_device + lo + lax.broadcasted_iota(jnp.int32, (count, 1), 0)
    return (rows >= 0) & (rows < total)


def pair_matrix(fine, coarse_first):
    if coarse_first:
        shape, fine_dim = (fine // 2, fine), 1
    else:
        shape, fine_dim = (fine, fine // 2), 0
    f_idx = lax.broadcasted_iota(jnp.int32, shape, fine_dim)
    c_idx = lax.broadcasted_iota(jnp.int32, shape, 1 - fine_dim)
    return jnp.where(jnp.right_shift(f_idx, 1) == c_idx, 1.0, 0.0).astype(jnp.bfloat16)


def split_dot(x, m):
    hi = x.astype(jnp.bfloat16)
    rest = x - hi.astype(jnp.float32)
    mid = rest.astype(jnp.bfloat16)
    lo = (rest - mid.astype(jnp.float32)).astype(jnp.bfloat16)
    out = jnp.dot(hi, m, preferred_element_type=jnp.float32)
    out = out + jnp.dot(mid, m, preferred_element_type=jnp.float32)
    return out + jnp.dot(lo, m, preferred_element_type=jnp.float32)


def put_blocks(ref, rows, value):
    for j in range(ref.shape[0]):
        ref[j, rows, :] = value[:, j * 128 : (j + 1) * 128]


def get_blocks(ref, rows):
    return jnp.concatenate([ref[j, rows, :] for j in range(ref.shape[0])], axis=1)


def sources(lo_ref, own_ref, hi_ref, slot):
    q = [
        jnp.concatenate([lo_ref[slot, layer], own_ref[slot, layer], hi_ref[slot, layer]], axis=0)
        for layer in range(2)
    ]
    return q, [-(0.5 * (q[0] + q[1])), -(0.5 * (q[0] - q[1]))]


def first_kernel(band_ref, lo_ref, own_ref, hi_ref, f1_ref, s1_ref, g1_ref, t_ref, r0_ref, r1_ref):
    band = band_ref[0]
    mask0 = row_mask(band, F0, -ROWS0, ROWS0, ROWS0 * 16)
    for slot in range(SLOTS):
        _, src = sources(lo_ref, own_ref, hi_ref, slot)
        for mode in range(2):
            d = diag(0, mode)
            s = src[mode]
            f0 = smoothing_weight * s / d
            f1 = smooth(f0, s, d, mask0)
            rows = pl.ds((2 * slot + mode) * F0, F0)
            f1_ref[rows, :] = f1
            put_blocks(r0_ref, rows, residual(f1, s, d, mask0))
    half = FIELDS * F1
    paired = get_blocks(r0_ref, pl.ds(0, half, stride=2)) + get_blocks(r0_ref, pl.ds(1, half, stride=2))
    s1_ref[...] = split_dot(paired, pair_matrix(COLS0, False))
    mask1 = row_mask(band, F1, -ROWS0 // 2, ROWS0 // 2, ROWS0 * 8)
    for field in range(FIELDS):
        d = diag(1, field % 2)
        rows = pl.ds(field * F1, F1)
        s = s1_ref[rows, :]
        g0 = smoothing_weight * s / d
        g1 = smooth(g0, s, d, mask1)
        g1_ref[rows, :] = g1
        put_blocks(r1_ref, rows, residual(g1, s, d, mask1))
    chunks = []
    for field in range(FIELDS):
        start = field * F1 + ROWS0 // 2
        chunks.append(
            get_blocks(r1_ref, pl.ds(start, CHUNK, stride=2))
            + get_blocks(r1_ref, pl.ds(start + 1, CHUNK, stride=2))
        )
    paired = jnp.concatenate(chunks, axis=0)
    keep = jnp.bitwise_and(lax.broadcasted_iota(jnp.int32, (FIELDS * CHUNK, 1), 0), CHUNK - 1) < ROWS0 // 4
    paired = jnp.where(keep, paired, 0.0)
    t_ref[...] = split_dot(paired, pair_matrix(COLS0 // 2, False))


def second_kernel(
    slots, band_ref, lo_ref, own_ref, hi_ref, f1_ref, s1_ref, g1_ref,
    tm2_ref, tm1_ref, t0_ref, tp1_ref, tp2_ref,
    out_ref,
    s2_ref, e2_ref, up1_ref, g4_ref, up0_ref,
):
    fields = 2 * slots
    band = band_ref[0]
    below = rolled(tm1_ref[...], CHUNK // 2, 0)
    above = rolled(tp1_ref[...], CHUNK // 2, 0)
    for field in range(fields):
        piece = pl.ds(field * CHUNK, CHUNK)
        base = field * F2
        s2_ref[pl.ds(base, CHUNK), :] = tm2_ref[piece, :] + below[field * CHUNK : (field + 1) * CHUNK]
        s2_ref[pl.ds(base + CHUNK, CHUNK), :] = t0_ref[piece, :] + above[field * CHUNK : (field + 1) * CHUNK]
        s2_ref[pl.ds(base + 2 * CHUNK, CHUNK), :] = tp2_ref[piece, :]
    mask2 = row_mask(band, F2, -CHUNK, ROWS0 // 4, ROWS0 * 4)
    for field in range(fields):
        d = diag(2, field % 2)
        rows = pl.ds(field * F2, F2)
        s = s2_ref[rows, :]
        e = smoothing_weight * s / d
        for repeat in range(COARSE_SWEEPS - 1):
            e = smooth(e, s, d, mask2)
        e2_ref[rows, :] = e
    cols = split_dot(e2_ref[...], pair_matrix(COLS0 // 2, True))
    n2 = fields * F2
    put_blocks(up1_ref, pl.ds(0, n2, stride=2), cols)
    put_blocks(up1_ref, pl.ds(1, n2, stride=2), cols)
    mask1 = row_mask(band, F1, -ROWS0 // 2, ROWS0 // 2, ROWS0 * 8)
    for field in range(fields):
        d = diag(1, field % 2)
        rows = pl.ds(field * F1, F1)
        s = s1_ref[rows, :]
        g2 = g1_ref[rows, :] + get_blocks(up1_ref, pl.ds(field * 2 * F2 + CHUNK, F1))
        g3 = smooth(g2, s, d, mask1)
        g4_ref[rows, :] = smooth(g3, s, d, mask1)
    cols = split_dot(g4_ref[...], pair_matrix(COLS0, True))
    n1 = fields * F1
    put_blocks(up0_ref, pl.ds(0, n1, stride=2), cols)
    put_blocks(up0_ref, pl.ds(1, n1, stride=2), cols)
    mask0 = row_mask(band, F0, -ROWS0, ROWS0, ROWS0 * 16)
    for slot in range(slots):
        q, src = sources(lo_ref, own_ref, hi_ref, slot)
        modes = []
        for mode in range(2):
            d = diag(0, mode)
            rows = pl.ds((2 * slot + mode) * F0, F0)
            f2 = f1_ref[rows, :] + get_blocks(up0_ref, rows)
            f3 = smooth(f2, src[mode], d, mask0)
            modes.append(smooth(f3, src[mode], d, mask0))
        streams = [modes[0] + modes[1], modes[0] - modes[1]]
        for layer in range(2):
            stream = streams[layer]
            pv = q[layer]
            stream_x = 0.5 * (rolled(stream, -1, 1) - rolled(stream, 1, 1))
            stream_y = 0.5 * (rolled(stream, -1, 0) - rolled(stream, 1, 0))
            vort_x = 0.5 * (rolled(pv, -1, 1) - rolled(pv, 1, 1))
            vort_y = 0.5 * (rolled(pv, -1, 0) - rolled(pv, 1, 0))
            laplace = stencil(stream) - 4.0 * stream
            drag = bottom_friction_coefficient if layer else 0.0
            jacobian = stream_x * vort_y - stream_y * vort_x
            new = pv - time_step * (jacobian + beta_slope * stream_x + drag * laplace)
            out_ref[slot, layer] = new[ROWS0 : 2 * ROWS0]


def vmem():
    return pl.BlockSpec(memory_space=pltpu.VMEM)


def smem():
    return pl.BlockSpec(memory_space=pltpu.SMEM)


PARAMS = pltpu.CompilerParams(vmem_limit_bytes=48 * 1024 * 1024)


def per_device(states, counts):
    group = lax.axis_index("particle")
    per_group = states.shape[0]
    totals = jnp.cumsum(counts, dtype=jnp.int32)
    slots = group * per_group + jnp.arange(per_group, dtype=jnp.int32)
    ancestor = jnp.sum(
        (totals[None, :] <= slots[:, None]).astype(jnp.int32), axis=1, dtype=jnp.int32
    )
    local_index = ancestor - (group * per_group - 1)

    band = lax.axis_index("band").astype(jnp.int32).reshape(1)
    lo_q = shifted(states, "band", 1)
    hi_q = shifted(states, "band", -1)
    f32 = jnp.float32
    f1, s1, g1, t = pl.pallas_call(
        first_kernel,
        out_shape=(
            jax.ShapeDtypeStruct((FIELDS * F0, COLS0), f32),
            jax.ShapeDtypeStruct((FIELDS * F1, COLS0 // 2), f32),
            jax.ShapeDtypeStruct((FIELDS * F1, COLS0 // 2), f32),
            jax.ShapeDtypeStruct((FIELDS * CHUNK, COLS0 // 4), f32),
        ),
        in_specs=[smem(), vmem(), vmem(), vmem()],
        out_specs=(vmem(), vmem(), vmem(), vmem()),
        scratch_shapes=[
            pltpu.VMEM((COLS0 // 128, FIELDS * F0, 128), f32),
            pltpu.VMEM((COLS0 // 256, FIELDS * F1, 128), f32),
        ],
        compiler_params=PARAMS,
    )(band, lo_q, states, hi_q)
    tm2 = shifted(t, "band", 2)
    tm1 = shifted(t, "band", 1)
    tp1 = shifted(t, "band", -1)
    tp2 = shifted(t, "band", -2)
    args = (band, lo_q, states, hi_q, f1, s1, g1, tm2, tm1, t, tp1, tp2)
    last = forecast_slots(SLOTS - 1, 1, args)
    below = shifted(last, "particle", 1)
    rest = forecast_slots(0, SLOTS - 1, args)
    picked = []
    for slot in range(SLOTS):
        index = local_index[slot]
        value = last[0]
        for k in range(SLOTS - 2, -1, -1):
            value = jnp.where(index == k + 1, rest[k], value)
        picked.append(jnp.where(index == 0, below[0], value))
    return jnp.stack(picked)


def forecast_slots(first, slots, args):
    fields = 2 * slots
    block = first // slots

    def rows(count, width):
        return pl.BlockSpec((count, width), lambda i: (block, 0))

    strips = pl.BlockSpec((slots, 2, ROWS0, COLS0), lambda i: (block, 0, 0, 0))
    in_specs = [smem(), strips, strips, strips,
                rows(fields * F0, COLS0), rows(fields * F1, COLS0 // 2), rows(fields * F1, COLS0 // 2)]
    in_specs += [rows(fields * CHUNK, COLS0 // 4)] * 5
    f32 = jnp.float32
    work = fields * F0 * COLS0 * 160
    return pl.pallas_call(
        functools.partial(second_kernel, slots),
        out_shape=jax.ShapeDtypeStruct((slots, 2, ROWS0, COLS0), f32),
        grid=(1,),
        in_specs=in_specs,
        out_specs=pl.BlockSpec((slots, 2, ROWS0, COLS0), lambda i: (0, 0, 0, 0)),
        scratch_shapes=[
            pltpu.VMEM((fields * F2, COLS0 // 4), f32),
            pltpu.VMEM((fields * F2, COLS0 // 4), f32),
            pltpu.VMEM((COLS0 // 256, 2 * fields * F2, 128), f32),
            pltpu.VMEM((fields * F1, COLS0 // 2), f32),
            pltpu.VMEM((COLS0 // 128, fields * F0, 128), f32),
        ],
        compiler_params=PARAMS,
        cost_estimate=pl.CostEstimate(flops=work, transcendentals=0, bytes_accessed=fields * F0 * COLS0 * 16),
    )(*args)


def solution(mesh):
    in_specs = (P("particle", None, "band", None), P())
    out_specs = P("particle", None, "band", None)
    return jax.shard_map(
        per_device, mesh=mesh, in_specs=in_specs, out_specs=out_specs, check_vma=False
    )
```

```python
import functools

import numpy as np
import jax
import jax.numpy as jnp
from jax import lax
from jax.experimental import pallas as pl
from jax.experimental.pallas import tpu as pltpu
from jax.sharding import PartitionSpec as P

GRID_HIERARCHY = 3
COARSE_SWEEPS = 6


smoothing_weight = 0.8
deform_term = 0.1
beta_slope = 0.5
bottom_friction_coefficient = 0.2
time_step = 0.5
meridional_weight = 1.8
zonal_weight = 0.2

SLOTS = 4
FIELDS = 2 * SLOTS
ROWS0 = 16
COLS0 = 1024
F0 = 3 * ROWS0
F1 = F0 // 2
F2 = F1
CHUNK = 8


def diag(level, mode):
    extra = np.float32(deform_term) * np.float32(4.0**level) if mode else np.float32(0.0)
    return float(np.float32(4.0) + extra)


def shifted(value, axis, steps):
    count = lax.axis_size(axis)
    first, last = (max(0, -steps), min(count, count - steps))
    return lax.ppermute(value, axis, [(source, source + steps) for source in range(first, last)])


def rolled(x, shift, axis):
    return pltpu.roll(x, shift % x.shape[axis], axis)


def stencil(f):
    up = rolled(f, -1, 0)
    down = rolled(f, 1, 0)
    along = rolled(f, -1, 1) + rolled(f, 1, 1)
    return meridional_weight * (up + down) + zonal_weight * along


def smooth(f, s, d, mask):
    applied = d * f - stencil(f)
    out = f + smoothing_weight * (s - applied) / d
    return jnp.where(mask, out, 0.0)


def residual(f, s, d, mask):
    return jnp.where(mask, s - (d * f - stencil(f)), 0.0)


def row_mask(band, count, lo, per_device, total):
    rows = band * per_device + lo + lax.broadcasted_iota(jnp.int32, (count, 1), 0)
    return (rows >= 0) & (rows < total)


def pair_matrix(fine, coarse_first):
    if coarse_first:
        shape, fine_dim = (fine // 2, fine), 1
    else:
        shape, fine_dim = (fine, fine // 2), 0
    f_idx = lax.broadcasted_iota(jnp.int32, shape, fine_dim)
    c_idx = lax.broadcasted_iota(jnp.int32, shape, 1 - fine_dim)
    return jnp.where(jnp.right_shift(f_idx, 1) == c_idx, 1.0, 0.0).astype(jnp.bfloat16)


def split_dot(x, m):
    hi = x.astype(jnp.bfloat16)
    rest = x - hi.astype(jnp.float32)
    mid = rest.astype(jnp.bfloat16)
    lo = (rest - mid.astype(jnp.float32)).astype(jnp.bfloat16)
    out = jnp.dot(hi, m, preferred_element_type=jnp.float32)
    out = out + jnp.dot(mid, m, preferred_element_type=jnp.float32)
    return out + jnp.dot(lo, m, preferred_element_type=jnp.float32)


def put_blocks(ref, rows, value):
    for j in range(ref.shape[0]):
        ref[j, rows, :] = value[:, j * 128 : (j + 1) * 128]


def get_blocks(ref, rows):
    return jnp.concatenate([ref[j, rows, :] for j in range(ref.shape[0])], axis=1)


def sources(lo_ref, own_ref, hi_ref, slot):
    q = [
        jnp.concatenate([lo_ref[slot, layer], own_ref[slot, layer], hi_ref[slot, layer]], axis=0)
        for layer in range(2)
    ]
    return q, [-(0.5 * (q[0] + q[1])), -(0.5 * (q[0] - q[1]))]


def first_kernel(band_ref, lo_ref, own_ref, hi_ref, f1_ref, s1_ref, g1_ref, t_ref, r0_ref, r1_ref):
    band = band_ref[0]
    mask0 = row_mask(band, F0, -ROWS0, ROWS0, ROWS0 * 16)
    for slot in range(SLOTS):
        _, src = sources(lo_ref, own_ref, hi_ref, slot)
        for mode in range(2):
            d = diag(0, mode)
            s = src[mode]
            f0 = smoothing_weight * s / d
            f1 = smooth(f0, s, d, mask0)
            rows = pl.ds((2 * slot + mode) * F0, F0)
            f1_ref[rows, :] = f1
            put_blocks(r0_ref, rows, residual(f1, s, d, mask0))
    half = FIELDS * F1
    paired = get_blocks(r0_ref, pl.ds(0, half, stride=2)) + get_blocks(r0_ref, pl.ds(1, half, stride=2))
    s1_ref[...] = split_dot(paired, pair_matrix(COLS0, False))
    mask1 = row_mask(band, F1, -ROWS0 // 2, ROWS0 // 2, ROWS0 * 8)
    for field in range(FIELDS):
        d = diag(1, field % 2)
        rows = pl.ds(field * F1, F1)
        s = s1_ref[rows, :]
        g0 = smoothing_weight * s / d
        g1 = smooth(g0, s, d, mask1)
        g1_ref[rows, :] = g1
        put_blocks(r1_ref, rows, residual(g1, s, d, mask1))
    chunks = []
    for field in range(FIELDS):
        start = field * F1 + ROWS0 // 2
        chunks.append(
            get_blocks(r1_ref, pl.ds(start, CHUNK, stride=2))
            + get_blocks(r1_ref, pl.ds(start + 1, CHUNK, stride=2))
        )
    paired = jnp.concatenate(chunks, axis=0)
    keep = jnp.bitwise_and(lax.broadcasted_iota(jnp.int32, (FIELDS * CHUNK, 1), 0), CHUNK - 1) < ROWS0 // 4
    paired = jnp.where(keep, paired, 0.0)
    t_ref[...] = split_dot(paired, pair_matrix(COLS0 // 2, False))


def second_kernel(
    slots, band_ref, lo_ref, own_ref, hi_ref, f1_ref, s1_ref, g1_ref,
    tm2_ref, tm1_ref, t0_ref, tp1_ref, tp2_ref,
    out_ref,
    s2_ref, e2_ref, up1_ref, g4_ref, up0_ref,
):
    fields = 2 * slots
    band = band_ref[0]
    below = rolled(tm1_ref[...], CHUNK // 2, 0)
    above = rolled(tp1_ref[...], CHUNK // 2, 0)
    for field in range(fields):
        piece = pl.ds(field * CHUNK, CHUNK)
        base = field * F2
        s2_ref[pl.ds(base, CHUNK), :] = tm2_ref[piece, :] + below[field * CHUNK : (field + 1) * CHUNK]
        s2_ref[pl.ds(base + CHUNK, CHUNK), :] = t0_ref[piece, :] + above[field * CHUNK : (field + 1) * CHUNK]
        s2_ref[pl.ds(base + 2 * CHUNK, CHUNK), :] = tp2_ref[piece, :]
    mask2 = row_mask(band, F2, -CHUNK, ROWS0 // 4, ROWS0 * 4)
    for field in range(fields):
        d = diag(2, field % 2)
        rows = pl.ds(field * F2, F2)
        s = s2_ref[rows, :]
        e = smoothing_weight * s / d
        for repeat in range(COARSE_SWEEPS - 1):
            e = smooth(e, s, d, mask2)
        e2_ref[rows, :] = e
    cols = split_dot(e2_ref[...], pair_matrix(COLS0 // 2, True))
    n2 = fields * F2
    put_blocks(up1_ref, pl.ds(0, n2, stride=2), cols)
    put_blocks(up1_ref, pl.ds(1, n2, stride=2), cols)
    mask1 = row_mask(band, F1, -ROWS0 // 2, ROWS0 // 2, ROWS0 * 8)
    for field in range(fields):
        d = diag(1, field % 2)
        rows = pl.ds(field * F1, F1)
        s = s1_ref[rows, :]
        g2 = g1_ref[rows, :] + get_blocks(up1_ref, pl.ds(field * 2 * F2 + CHUNK, F1))
        g3 = smooth(g2, s, d, mask1)
        g4_ref[rows, :] = smooth(g3, s, d, mask1)
    cols = split_dot(g4_ref[...], pair_matrix(COLS0, True))
    n1 = fields * F1
    put_blocks(up0_ref, pl.ds(0, n1, stride=2), cols)
    put_blocks(up0_ref, pl.ds(1, n1, stride=2), cols)
    mask0 = row_mask(band, F0, -ROWS0, ROWS0, ROWS0 * 16)
    for slot in range(slots):
        q, src = sources(lo_ref, own_ref, hi_ref, slot)
        modes = []
        for mode in range(2):
            d = diag(0, mode)
            rows = pl.ds((2 * slot + mode) * F0, F0)
            f2 = f1_ref[rows, :] + get_blocks(up0_ref, rows)
            f3 = smooth(f2, src[mode], d, mask0)
            modes.append(smooth(f3, src[mode], d, mask0))
        streams = [modes[0] + modes[1], modes[0] - modes[1]]
        for layer in range(2):
            stream = streams[layer]
            pv = q[layer]
            stream_x = 0.5 * (rolled(stream, -1, 1) - rolled(stream, 1, 1))
            stream_y = 0.5 * (rolled(stream, -1, 0) - rolled(stream, 1, 0))
            vort_x = 0.5 * (rolled(pv, -1, 1) - rolled(pv, 1, 1))
            vort_y = 0.5 * (rolled(pv, -1, 0) - rolled(pv, 1, 0))
            laplace = stencil(stream) - 4.0 * stream
            drag = bottom_friction_coefficient if layer else 0.0
            jacobian = stream_x * vort_y - stream_y * vort_x
            new = pv - time_step * (jacobian + beta_slope * stream_x + drag * laplace)
            out_ref[slot, layer] = new[ROWS0 : 2 * ROWS0]


def pick_kernel(index_ref, below_ref, last_ref, rest_ref, out_ref, sems):
    choices = [below_ref.at[0]] + [rest_ref.at[k] for k in range(SLOTS - 1)] + [last_ref.at[0]]
    for slot in range(SLOTS):
        index = index_ref[slot]
        last = len(choices) - 1
        for k, source in enumerate(choices):
            hit = index <= 0 if k == 0 else (index >= last if k == last else index == k)

            @pl.when(hit)
            def _():
                pltpu.make_async_copy(source, out_ref.at[slot], sems.at[slot]).start()
    for slot in range(SLOTS):
        pltpu.make_async_copy(choices[0], out_ref.at[slot], sems.at[slot]).wait()


def vmem():
    return pl.BlockSpec(memory_space=pltpu.VMEM)


def hbm():
    return pl.BlockSpec(memory_space=pl.ANY)


def smem():
    return pl.BlockSpec(memory_space=pltpu.SMEM)


PARAMS = pltpu.CompilerParams(vmem_limit_bytes=48 * 1024 * 1024)


def per_device(states, counts):
    group = lax.axis_index("particle")
    per_group = states.shape[0]
    totals = jnp.cumsum(counts, dtype=jnp.int32)
    slots = group * per_group + jnp.arange(per_group, dtype=jnp.int32)
    ancestor = jnp.sum(
        (totals[None, :] <= slots[:, None]).astype(jnp.int32), axis=1, dtype=jnp.int32
    )
    local_index = ancestor - (group * per_group - 1)

    band = lax.axis_index("band").astype(jnp.int32).reshape(1)
    lo_q = shifted(states, "band", 1)
    hi_q = shifted(states, "band", -1)
    f32 = jnp.float32
    f1, s1, g1, t = pl.pallas_call(
        first_kernel,
        out_shape=(
            jax.ShapeDtypeStruct((FIELDS * F0, COLS0), f32),
            jax.ShapeDtypeStruct((FIELDS * F1, COLS0 // 2), f32),
            jax.ShapeDtypeStruct((FIELDS * F1, COLS0 // 2), f32),
            jax.ShapeDtypeStruct((FIELDS * CHUNK, COLS0 // 4), f32),
        ),
        in_specs=[smem(), vmem(), vmem(), vmem()],
        out_specs=(vmem(), vmem(), vmem(), vmem()),
        scratch_shapes=[
            pltpu.VMEM((COLS0 // 128, FIELDS * F0, 128), f32),
            pltpu.VMEM((COLS0 // 256, FIELDS * F1, 128), f32),
        ],
        compiler_params=PARAMS,
    )(band, lo_q, states, hi_q)
    tm2 = shifted(t, "band", 2)
    tm1 = shifted(t, "band", 1)
    tp1 = shifted(t, "band", -1)
    tp2 = shifted(t, "band", -2)
    args = (band, lo_q, states, hi_q, f1, s1, g1, tm2, tm1, t, tp1, tp2)
    last = forecast_slots(SLOTS - 1, 1, args)
    below = shifted(last, "particle", 1)
    rest = forecast_slots(0, SLOTS - 1, args)
    return pl.pallas_call(
        pick_kernel,
        out_shape=jax.ShapeDtypeStruct(states.shape, f32),
        in_specs=[smem(), hbm(), hbm(), hbm()],
        out_specs=hbm(),
        scratch_shapes=[pltpu.SemaphoreType.DMA((SLOTS,))],
    )(local_index, below, last, rest)


def forecast_slots(first, slots, args):
    fields = 2 * slots
    block = first // slots

    def rows(count, width):
        return pl.BlockSpec((count, width), lambda i: (block, 0))

    strips = pl.BlockSpec((slots, 2, ROWS0, COLS0), lambda i: (block, 0, 0, 0))
    in_specs = [smem(), strips, strips, strips,
                rows(fields * F0, COLS0), rows(fields * F1, COLS0 // 2), rows(fields * F1, COLS0 // 2)]
    in_specs += [rows(fields * CHUNK, COLS0 // 4)] * 5
    f32 = jnp.float32
    work = fields * F0 * COLS0 * 160
    return pl.pallas_call(
        functools.partial(second_kernel, slots),
        out_shape=jax.ShapeDtypeStruct((slots, 2, ROWS0, COLS0), f32),
        grid=(1,),
        in_specs=in_specs,
        out_specs=pl.BlockSpec((slots, 2, ROWS0, COLS0), lambda i: (0, 0, 0, 0)),
        scratch_shapes=[
            pltpu.VMEM((fields * F2, COLS0 // 4), f32),
            pltpu.VMEM((fields * F2, COLS0 // 4), f32),
            pltpu.VMEM((COLS0 // 256, 2 * fields * F2, 128), f32),
            pltpu.VMEM((fields * F1, COLS0 // 2), f32),
            pltpu.VMEM((COLS0 // 128, fields * F0, 128), f32),
        ],
        compiler_params=PARAMS,
        cost_estimate=pl.CostEstimate(flops=work, transcendentals=0, bytes_accessed=fields * F0 * COLS0 * 16),
    )(*args)


def solution(mesh):
    in_specs = (P("particle", None, "band", None), P())
    out_specs = P("particle", None, "band", None)
    return jax.shard_map(
        per_device, mesh=mesh, in_specs=in_specs, out_specs=out_specs, check_vma=False
    )
```

```python
import functools

import numpy as np
import jax
import jax.numpy as jnp
from jax import lax
from jax.experimental import pallas as pl
from jax.experimental.pallas import tpu as pltpu
from jax.sharding import PartitionSpec as P

GRID_HIERARCHY = 3
COARSE_SWEEPS = 6


smoothing_weight = 0.8
deform_term = 0.1
beta_slope = 0.5
bottom_friction_coefficient = 0.2
time_step = 0.5
meridional_weight = 1.8
zonal_weight = 0.2

SLOTS = 4
FIELDS = 2 * SLOTS
ROWS0 = 16
COLS0 = 1024
F0 = 3 * ROWS0
F1 = F0 // 2
F2 = F1
CHUNK = 8


def diag(level, mode):
    extra = np.float32(deform_term) * np.float32(4.0**level) if mode else np.float32(0.0)
    return float(np.float32(4.0) + extra)


def shifted(value, axis, steps):
    count = lax.axis_size(axis)
    first, last = (max(0, -steps), min(count, count - steps))
    return lax.ppermute(value, axis, [(source, source + steps) for source in range(first, last)])


def rolled(x, shift, axis):
    return pltpu.roll(x, shift % x.shape[axis], axis)


def stencil(f):
    up = rolled(f, -1, 0)
    down = rolled(f, 1, 0)
    along = rolled(f, -1, 1) + rolled(f, 1, 1)
    return meridional_weight * (up + down) + zonal_weight * along


def smooth(f, s, d, mask):
    applied = d * f - stencil(f)
    out = f + smoothing_weight * (s - applied) / d
    return jnp.where(mask, out, 0.0)


def residual(f, s, d, mask):
    return jnp.where(mask, s - (d * f - stencil(f)), 0.0)


def row_mask(band, count, lo, per_device, total):
    rows = band * per_device + lo + lax.broadcasted_iota(jnp.int32, (count, 1), 0)
    return (rows >= 0) & (rows < total)


def pair_matrix(fine, coarse_first):
    if coarse_first:
        shape, fine_dim = (fine // 2, fine), 1
    else:
        shape, fine_dim = (fine, fine // 2), 0
    f_idx = lax.broadcasted_iota(jnp.int32, shape, fine_dim)
    c_idx = lax.broadcasted_iota(jnp.int32, shape, 1 - fine_dim)
    return jnp.where(jnp.right_shift(f_idx, 1) == c_idx, 1.0, 0.0).astype(jnp.bfloat16)


def split_dot(x, m):
    hi = x.astype(jnp.bfloat16)
    rest = x - hi.astype(jnp.float32)
    mid = rest.astype(jnp.bfloat16)
    lo = (rest - mid.astype(jnp.float32)).astype(jnp.bfloat16)
    out = jnp.dot(hi, m, preferred_element_type=jnp.float32)
    out = out + jnp.dot(mid, m, preferred_element_type=jnp.float32)
    return out + jnp.dot(lo, m, preferred_element_type=jnp.float32)


def put_blocks(ref, rows, value):
    for j in range(ref.shape[0]):
        ref[j, rows, :] = value[:, j * 128 : (j + 1) * 128]


def get_blocks(ref, rows):
    return jnp.concatenate([ref[j, rows, :] for j in range(ref.shape[0])], axis=1)


def sources(lo_ref, own_ref, hi_ref, slot):
    q = [
        jnp.concatenate([lo_ref[slot, layer], own_ref[slot, layer], hi_ref[slot, layer]], axis=0)
        for layer in range(2)
    ]
    return q, [-(0.5 * (q[0] + q[1])), -(0.5 * (q[0] - q[1]))]


def first_kernel(band_ref, lo_ref, own_ref, hi_ref, f1_ref, s1_ref, g1_ref, t_ref, r0_ref, r1_ref):
    band = band_ref[0]
    mask0 = row_mask(band, F0, -ROWS0, ROWS0, ROWS0 * 16)
    for slot in range(SLOTS):
        _, src = sources(lo_ref, own_ref, hi_ref, slot)
        for mode in range(2):
            d = diag(0, mode)
            s = src[mode]
            f0 = smoothing_weight * s / d
            f1 = smooth(f0, s, d, mask0)
            rows = pl.ds((2 * slot + mode) * F0, F0)
            f1_ref[rows, :] = f1
            put_blocks(r0_ref, rows, residual(f1, s, d, mask0))
    half = FIELDS * F1
    paired = get_blocks(r0_ref, pl.ds(0, half, stride=2)) + get_blocks(r0_ref, pl.ds(1, half, stride=2))
    s1_ref[...] = split_dot(paired, pair_matrix(COLS0, False))
    mask1 = row_mask(band, F1, -ROWS0 // 2, ROWS0 // 2, ROWS0 * 8)
    for field in range(FIELDS):
        d = diag(1, field % 2)
        rows = pl.ds(field * F1, F1)
        s = s1_ref[rows, :]
        g0 = smoothing_weight * s / d
        g1 = smooth(g0, s, d, mask1)
        g1_ref[rows, :] = g1
        put_blocks(r1_ref, rows, residual(g1, s, d, mask1))
    chunks = []
    for field in range(FIELDS):
        start = field * F1 + ROWS0 // 2
        chunks.append(
            get_blocks(r1_ref, pl.ds(start, CHUNK, stride=2))
            + get_blocks(r1_ref, pl.ds(start + 1, CHUNK, stride=2))
        )
    paired = jnp.concatenate(chunks, axis=0)
    keep = jnp.bitwise_and(lax.broadcasted_iota(jnp.int32, (FIELDS * CHUNK, 1), 0), CHUNK - 1) < ROWS0 // 4
    paired = jnp.where(keep, paired, 0.0)
    t_ref[...] = split_dot(paired, pair_matrix(COLS0 // 2, False))


def second_kernel(
    slots, picks, *refs):
    if picks:
        (index_ref, band_ref, lo_ref, own_ref, hi_ref, f1_ref, s1_ref, g1_ref,
         tm2_ref, tm1_ref, t0_ref, tp1_ref, tp2_ref, last_ref,
         out_ref, s2_ref, e2_ref, up1_ref, g4_ref, up0_ref, own_out) = refs
    else:
        (band_ref, lo_ref, own_ref, hi_ref, f1_ref, s1_ref, g1_ref,
         tm2_ref, tm1_ref, t0_ref, tp1_ref, tp2_ref,
         out_ref, s2_ref, e2_ref, up1_ref, g4_ref, up0_ref) = refs
        own_out = out_ref
    fields = 2 * slots
    band = band_ref[0]
    below = rolled(tm1_ref[...], CHUNK // 2, 0)
    above = rolled(tp1_ref[...], CHUNK // 2, 0)
    for field in range(fields):
        piece = pl.ds(field * CHUNK, CHUNK)
        base = field * F2
        s2_ref[pl.ds(base, CHUNK), :] = tm2_ref[piece, :] + below[field * CHUNK : (field + 1) * CHUNK]
        s2_ref[pl.ds(base + CHUNK, CHUNK), :] = t0_ref[piece, :] + above[field * CHUNK : (field + 1) * CHUNK]
        s2_ref[pl.ds(base + 2 * CHUNK, CHUNK), :] = tp2_ref[piece, :]
    mask2 = row_mask(band, F2, -CHUNK, ROWS0 // 4, ROWS0 * 4)
    for field in range(fields):
        d = diag(2, field % 2)
        rows = pl.ds(field * F2, F2)
        s = s2_ref[rows, :]
        e = smoothing_weight * s / d
        for repeat in range(COARSE_SWEEPS - 1):
            e = smooth(e, s, d, mask2)
        e2_ref[rows, :] = e
    cols = split_dot(e2_ref[...], pair_matrix(COLS0 // 2, True))
    n2 = fields * F2
    put_blocks(up1_ref, pl.ds(0, n2, stride=2), cols)
    put_blocks(up1_ref, pl.ds(1, n2, stride=2), cols)
    mask1 = row_mask(band, F1, -ROWS0 // 2, ROWS0 // 2, ROWS0 * 8)
    for field in range(fields):
        d = diag(1, field % 2)
        rows = pl.ds(field * F1, F1)
        s = s1_ref[rows, :]
        g2 = g1_ref[rows, :] + get_blocks(up1_ref, pl.ds(field * 2 * F2 + CHUNK, F1))
        g3 = smooth(g2, s, d, mask1)
        g4_ref[rows, :] = smooth(g3, s, d, mask1)
    cols = split_dot(g4_ref[...], pair_matrix(COLS0, True))
    n1 = fields * F1
    put_blocks(up0_ref, pl.ds(0, n1, stride=2), cols)
    put_blocks(up0_ref, pl.ds(1, n1, stride=2), cols)
    mask0 = row_mask(band, F0, -ROWS0, ROWS0, ROWS0 * 16)
    for slot in range(slots):
        q, src = sources(lo_ref, own_ref, hi_ref, slot)
        modes = []
        for mode in range(2):
            d = diag(0, mode)
            rows = pl.ds((2 * slot + mode) * F0, F0)
            f2 = f1_ref[rows, :] + get_blocks(up0_ref, rows)
            f3 = smooth(f2, src[mode], d, mask0)
            modes.append(smooth(f3, src[mode], d, mask0))
        streams = [modes[0] + modes[1], modes[0] - modes[1]]
        for layer in range(2):
            stream = streams[layer]
            pv = q[layer]
            stream_x = 0.5 * (rolled(stream, -1, 1) - rolled(stream, 1, 1))
            stream_y = 0.5 * (rolled(stream, -1, 0) - rolled(stream, 1, 0))
            vort_x = 0.5 * (rolled(pv, -1, 1) - rolled(pv, 1, 1))
            vort_y = 0.5 * (rolled(pv, -1, 0) - rolled(pv, 1, 0))
            laplace = stencil(stream) - 4.0 * stream
            drag = bottom_friction_coefficient if layer else 0.0
            jacobian = stream_x * vort_y - stream_y * vort_x
            new = pv - time_step * (jacobian + beta_slope * stream_x + drag * laplace)
            own_out[slot, layer] = new[ROWS0 : 2 * ROWS0]
    if picks:
        pick_slots(index_ref, own_out, last_ref, out_ref)


def pick_slots(index_ref, rest_ref, last_ref, out_ref):
    for slot in range(SLOTS):
        index = index_ref[slot]
        value = last_ref[0]
        for k in range(SLOTS - 2, -1, -1):
            value = jnp.where(index == k + 1, rest_ref[k], value)
        out_ref[slot] = value


def fix_kernel(index_ref, below_ref, current_ref, out_ref):
    out_ref[0] = jnp.where(index_ref[0] <= 0, below_ref[0], current_ref[0])


def vmem():
    return pl.BlockSpec(memory_space=pltpu.VMEM)


def smem():
    return pl.BlockSpec(memory_space=pltpu.SMEM)


PARAMS = pltpu.CompilerParams(vmem_limit_bytes=48 * 1024 * 1024)


def per_device(states, counts):
    group = lax.axis_index("particle")
    per_group = states.shape[0]
    totals = jnp.cumsum(counts, dtype=jnp.int32)
    slots = group * per_group + jnp.arange(per_group, dtype=jnp.int32)
    ancestor = jnp.sum(
        (totals[None, :] <= slots[:, None]).astype(jnp.int32), axis=1, dtype=jnp.int32
    )
    local_index = ancestor - (group * per_group - 1)

    band = lax.axis_index("band").astype(jnp.int32).reshape(1)
    lo_q = shifted(states, "band", 1)
    hi_q = shifted(states, "band", -1)
    f32 = jnp.float32
    f1, s1, g1, t = pl.pallas_call(
        first_kernel,
        out_shape=(
            jax.ShapeDtypeStruct((FIELDS * F0, COLS0), f32),
            jax.ShapeDtypeStruct((FIELDS * F1, COLS0 // 2), f32),
            jax.ShapeDtypeStruct((FIELDS * F1, COLS0 // 2), f32),
            jax.ShapeDtypeStruct((FIELDS * CHUNK, COLS0 // 4), f32),
        ),
        in_specs=[smem(), vmem(), vmem(), vmem()],
        out_specs=(vmem(), vmem(), vmem(), vmem()),
        scratch_shapes=[
            pltpu.VMEM((COLS0 // 128, FIELDS * F0, 128), f32),
            pltpu.VMEM((COLS0 // 256, FIELDS * F1, 128), f32),
        ],
        compiler_params=PARAMS,
    )(band, lo_q, states, hi_q)
    tm2 = shifted(t, "band", 2)
    tm1 = shifted(t, "band", 1)
    tp1 = shifted(t, "band", -1)
    tp2 = shifted(t, "band", -2)
    args = (band, lo_q, states, hi_q, f1, s1, g1, tm2, tm1, t, tp1, tp2)
    last = forecast_slots(SLOTS - 1, 1, args)
    below = shifted(last, "particle", 1)
    picked = forecast_slots(0, SLOTS - 1, args, (local_index, last))
    strip = pl.BlockSpec((1, 2, ROWS0, COLS0), lambda i: (0, 0, 0, 0))
    return pl.pallas_call(
        fix_kernel,
        out_shape=jax.ShapeDtypeStruct(states.shape, f32),
        grid=(1,),
        in_specs=[smem(), strip, strip],
        out_specs=strip,
        input_output_aliases={2: 0},
    )(local_index, below, picked)


def forecast_slots(first, slots, args, pick=None):
    fields = 2 * slots
    block = first // slots

    def rows(count, width):
        return pl.BlockSpec((count, width), lambda i: (block, 0))

    strips = pl.BlockSpec((slots, 2, ROWS0, COLS0), lambda i: (block, 0, 0, 0))
    in_specs = [smem(), strips, strips, strips,
                rows(fields * F0, COLS0), rows(fields * F1, COLS0 // 2), rows(fields * F1, COLS0 // 2)]
    in_specs += [rows(fields * CHUNK, COLS0 // 4)] * 5
    f32 = jnp.float32
    out_shape = jax.ShapeDtypeStruct((slots, 2, ROWS0, COLS0), f32)
    out_spec = pl.BlockSpec((slots, 2, ROWS0, COLS0), lambda i: (0, 0, 0, 0))
    extra_scratch = []
    if pick is not None:
        whole = pl.BlockSpec((SLOTS, 2, ROWS0, COLS0), lambda i: (0, 0, 0, 0))
        in_specs = [smem()] + in_specs + [pl.BlockSpec((1, 2, ROWS0, COLS0), lambda i: (0, 0, 0, 0))]
        args = (pick[0],) + tuple(args) + (pick[1],)
        out_shape = jax.ShapeDtypeStruct((SLOTS, 2, ROWS0, COLS0), f32)
        out_spec = whole
        extra_scratch = [pltpu.VMEM((slots, 2, ROWS0, COLS0), f32)]
    work = fields * F0 * COLS0 * 160
    return pl.pallas_call(
        functools.partial(second_kernel, slots, pick is not None),
        out_shape=out_shape,
        grid=(1,),
        in_specs=in_specs,
        out_specs=out_spec,
        scratch_shapes=[
            pltpu.VMEM((fields * F2, COLS0 // 4), f32),
            pltpu.VMEM((fields * F2, COLS0 // 4), f32),
            pltpu.VMEM((COLS0 // 256, 2 * fields * F2, 128), f32),
            pltpu.VMEM((fields * F1, COLS0 // 2), f32),
            pltpu.VMEM((COLS0 // 128, fields * F0, 128), f32),
        ] + extra_scratch,
        compiler_params=PARAMS,
        cost_estimate=pl.CostEstimate(flops=work, transcendentals=0, bytes_accessed=fields * F0 * COLS0 * 16),
    )(*args)


def solution(mesh):
    in_specs = (P("particle", None, "band", None), P())
    out_specs = P("particle", None, "band", None)
    return jax.shard_map(
        per_device, mesh=mesh, in_specs=in_specs, out_specs=out_specs, check_vma=False
    )
```

```python
import functools

import numpy as np
import jax
import jax.numpy as jnp
from jax import lax
from jax.experimental import pallas as pl
from jax.experimental.pallas import tpu as pltpu
from jax.sharding import PartitionSpec as P

GRID_HIERARCHY = 3
COARSE_SWEEPS = 6


smoothing_weight = 0.8
deform_term = 0.1
beta_slope = 0.5
bottom_friction_coefficient = 0.2
time_step = 0.5
meridional_weight = 1.8
zonal_weight = 0.2

SLOTS = 4
FIELDS = 2 * SLOTS
ROWS0 = 16
COLS0 = 1024
F0 = 3 * ROWS0
F1 = F0 // 2
F2 = F1
CHUNK = 8


def diag(level, mode):
    extra = np.float32(deform_term) * np.float32(4.0**level) if mode else np.float32(0.0)
    return float(np.float32(4.0) + extra)


def shifted(value, axis, steps):
    count = lax.axis_size(axis)
    first, last = (max(0, -steps), min(count, count - steps))
    return lax.ppermute(value, axis, [(source, source + steps) for source in range(first, last)])


def rolled(x, shift, axis):
    return pltpu.roll(x, shift % x.shape[axis], axis)


def stencil(f):
    up = rolled(f, -1, 0)
    down = rolled(f, 1, 0)
    along = rolled(f, -1, 1) + rolled(f, 1, 1)
    return meridional_weight * (up + down) + zonal_weight * along


def smooth(f, s, d, mask):
    applied = d * f - stencil(f)
    out = f + smoothing_weight * (s - applied) / d
    return jnp.where(mask, out, 0.0)


def residual(f, s, d, mask):
    return jnp.where(mask, s - (d * f - stencil(f)), 0.0)


def row_mask(band, count, lo, per_device, total):
    rows = band * per_device + lo + lax.broadcasted_iota(jnp.int32, (count, 1), 0)
    return (rows >= 0) & (rows < total)


def pair_matrix(fine, coarse_first):
    if coarse_first:
        shape, fine_dim = (fine // 2, fine), 1
    else:
        shape, fine_dim = (fine, fine // 2), 0
    f_idx = lax.broadcasted_iota(jnp.int32, shape, fine_dim)
    c_idx = lax.broadcasted_iota(jnp.int32, shape, 1 - fine_dim)
    return jnp.where(jnp.right_shift(f_idx, 1) == c_idx, 1.0, 0.0).astype(jnp.bfloat16)


def split_dot(x, m):
    hi = x.astype(jnp.bfloat16)
    rest = x - hi.astype(jnp.float32)
    mid = rest.astype(jnp.bfloat16)
    lo = (rest - mid.astype(jnp.float32)).astype(jnp.bfloat16)
    out = jnp.dot(hi, m, preferred_element_type=jnp.float32)
    out = out + jnp.dot(mid, m, preferred_element_type=jnp.float32)
    return out + jnp.dot(lo, m, preferred_element_type=jnp.float32)


def put_blocks(ref, rows, value):
    for j in range(ref.shape[0]):
        ref[j, rows, :] = value[:, j * 128 : (j + 1) * 128]


def get_blocks(ref, rows):
    return jnp.concatenate([ref[j, rows, :] for j in range(ref.shape[0])], axis=1)


HALO = 12


def halo_window(ref, piece, below):
    start = HALO * piece
    if (piece % 2 == 1) == below:
        window = ref[pl.ds(start - 4 if below else start, ROWS0), :]
        return window
    window = ref[pl.ds(start if below else start - 4, ROWS0), :]
    return rolled(window, 4 if below else -4, 0)


def sources(lo_ref, own_ref, hi_ref, slot):
    q = [
        jnp.concatenate(
            [
                halo_window(lo_ref, 2 * slot + layer, True),
                own_ref[slot, layer],
                halo_window(hi_ref, 2 * slot + layer, False),
            ],
            axis=0,
        )
        for layer in range(2)
    ]
    return q, [-(0.5 * (q[0] + q[1])), -(0.5 * (q[0] - q[1]))]


def first_kernel(band_ref, lo_ref, own_ref, hi_ref, f1_ref, s1_ref, g1_ref, t_ref, r0_ref, r1_ref):
    band = band_ref[0]
    mask0 = row_mask(band, F0, -ROWS0, ROWS0, ROWS0 * 16)
    for slot in range(SLOTS):
        _, src = sources(lo_ref, own_ref, hi_ref, slot)
        for mode in range(2):
            d = diag(0, mode)
            s = src[mode]
            f0 = smoothing_weight * s / d
            f1 = smooth(f0, s, d, mask0)
            rows = pl.ds((2 * slot + mode) * F0, F0)
            f1_ref[rows, :] = f1
            put_blocks(r0_ref, rows, residual(f1, s, d, mask0))
    half = FIELDS * F1
    paired = get_blocks(r0_ref, pl.ds(0, half, stride=2)) + get_blocks(r0_ref, pl.ds(1, half, stride=2))
    s1_ref[...] = split_dot(paired, pair_matrix(COLS0, False))
    mask1 = row_mask(band, F1, -ROWS0 // 2, ROWS0 // 2, ROWS0 * 8)
    for field in range(FIELDS):
        d = diag(1, field % 2)
        rows = pl.ds(field * F1, F1)
        s = s1_ref[rows, :]
        g0 = smoothing_weight * s / d
        g1 = smooth(g0, s, d, mask1)
        g1_ref[rows, :] = g1
        put_blocks(r1_ref, rows, residual(g1, s, d, mask1))
    chunks = []
    for field in range(FIELDS):
        start = field * F1 + ROWS0 // 2
        chunks.append(
            get_blocks(r1_ref, pl.ds(start, CHUNK, stride=2))
            + get_blocks(r1_ref, pl.ds(start + 1, CHUNK, stride=2))
        )
    paired = jnp.concatenate(chunks, axis=0)
    keep = jnp.bitwise_and(lax.broadcasted_iota(jnp.int32, (FIELDS * CHUNK, 1), 0), CHUNK - 1) < ROWS0 // 4
    paired = jnp.where(keep, paired, 0.0)
    t_ref[...] = split_dot(paired, pair_matrix(COLS0 // 2, False))


def second_kernel(
    slots, picks, *refs):
    if picks:
        (index_ref, band_ref, lo_ref, own_ref, hi_ref, f1_ref, s1_ref, g1_ref,
         tm2_ref, tm1_ref, t0_ref, tp1_ref, tp2_ref, last_ref,
         out_ref, s2_ref, e2_ref, up1_ref, g4_ref, up0_ref, own_out) = refs
    else:
        (band_ref, lo_ref, own_ref, hi_ref, f1_ref, s1_ref, g1_ref,
         tm2_ref, tm1_ref, t0_ref, tp1_ref, tp2_ref,
         out_ref, s2_ref, e2_ref, up1_ref, g4_ref, up0_ref) = refs
        own_out = out_ref
    fields = 2 * slots
    band = band_ref[0]
    below = rolled(tm1_ref[...], CHUNK // 2, 0)
    above = rolled(tp1_ref[...], CHUNK // 2, 0)
    for field in range(fields):
        piece = pl.ds(field * CHUNK, CHUNK)
        base = field * F2
        s2_ref[pl.ds(base, CHUNK), :] = tm2_ref[piece, :] + below[field * CHUNK : (field + 1) * CHUNK]
        s2_ref[pl.ds(base + CHUNK, CHUNK), :] = t0_ref[piece, :] + above[field * CHUNK : (field + 1) * CHUNK]
        s2_ref[pl.ds(base + 2 * CHUNK, CHUNK), :] = tp2_ref[piece, :]
    mask2 = row_mask(band, F2, -CHUNK, ROWS0 // 4, ROWS0 * 4)
    for field in range(fields):
        d = diag(2, field % 2)
        rows = pl.ds(field * F2, F2)
        s = s2_ref[rows, :]
        e = smoothing_weight * s / d
        for repeat in range(COARSE_SWEEPS - 1):
            e = smooth(e, s, d, mask2)
        e2_ref[rows, :] = e
    cols = split_dot(e2_ref[...], pair_matrix(COLS0 // 2, True))
    n2 = fields * F2
    put_blocks(up1_ref, pl.ds(0, n2, stride=2), cols)
    put_blocks(up1_ref, pl.ds(1, n2, stride=2), cols)
    mask1 = row_mask(band, F1, -ROWS0 // 2, ROWS0 // 2, ROWS0 * 8)
    for field in range(fields):
        d = diag(1, field % 2)
        rows = pl.ds(field * F1, F1)
        s = s1_ref[rows, :]
        g2 = g1_ref[rows, :] + get_blocks(up1_ref, pl.ds(field * 2 * F2 + CHUNK, F1))
        g3 = smooth(g2, s, d, mask1)
        g4_ref[rows, :] = smooth(g3, s, d, mask1)
    cols = split_dot(g4_ref[...], pair_matrix(COLS0, True))
    n1 = fields * F1
    put_blocks(up0_ref, pl.ds(0, n1, stride=2), cols)
    put_blocks(up0_ref, pl.ds(1, n1, stride=2), cols)
    mask0 = row_mask(band, F0, -ROWS0, ROWS0, ROWS0 * 16)
    for slot in range(slots):
        q, src = sources(lo_ref, own_ref, hi_ref, slot)
        modes = []
        for mode in range(2):
            d = diag(0, mode)
            rows = pl.ds((2 * slot + mode) * F0, F0)
            f2 = f1_ref[rows, :] + get_blocks(up0_ref, rows)
            f3 = smooth(f2, src[mode], d, mask0)
            modes.append(smooth(f3, src[mode], d, mask0))
        streams = [modes[0] + modes[1], modes[0] - modes[1]]
        for layer in range(2):
            stream = streams[layer]
            pv = q[layer]
            stream_x = 0.5 * (rolled(stream, -1, 1) - rolled(stream, 1, 1))
            stream_y = 0.5 * (rolled(stream, -1, 0) - rolled(stream, 1, 0))
            vort_x = 0.5 * (rolled(pv, -1, 1) - rolled(pv, 1, 1))
            vort_y = 0.5 * (rolled(pv, -1, 0) - rolled(pv, 1, 0))
            laplace = stencil(stream) - 4.0 * stream
            drag = bottom_friction_coefficient if layer else 0.0
            jacobian = stream_x * vort_y - stream_y * vort_x
            new = pv - time_step * (jacobian + beta_slope * stream_x + drag * laplace)
            own_out[slot, layer] = new[ROWS0 : 2 * ROWS0]
    if picks:
        pick_slots(index_ref, own_out, last_ref, out_ref)


def pick_slots(index_ref, rest_ref, last_ref, out_ref):
    for slot in range(SLOTS):
        index = index_ref[slot]
        value = last_ref[0]
        for k in range(SLOTS - 2, -1, -1):
            value = jnp.where(index == k + 1, rest_ref[k], value)
        out_ref[slot] = value


def fix_kernel(index_ref, below_ref, current_ref, out_ref):
    out_ref[0] = jnp.where(index_ref[0] <= 0, below_ref[0], current_ref[0])


def vmem():
    return pl.BlockSpec(memory_space=pltpu.VMEM)


def smem():
    return pl.BlockSpec(memory_space=pltpu.SMEM)


PARAMS = pltpu.CompilerParams(vmem_limit_bytes=48 * 1024 * 1024)


def per_device(states, counts):
    group = lax.axis_index("particle")
    per_group = states.shape[0]
    totals = jnp.cumsum(counts, dtype=jnp.int32)
    slots = group * per_group + jnp.arange(per_group, dtype=jnp.int32)
    ancestor = jnp.sum(
        (totals[None, :] <= slots[:, None]).astype(jnp.int32), axis=1, dtype=jnp.int32
    )
    local_index = ancestor - (group * per_group - 1)

    band = lax.axis_index("band").astype(jnp.int32).reshape(1)
    pieces = states.shape[0] * states.shape[1] * HALO
    lo_q = shifted(states[:, :, ROWS0 - HALO :, :].reshape(pieces, COLS0), "band", 1)
    hi_q = shifted(states[:, :, :HALO, :].reshape(pieces, COLS0), "band", -1)
    f32 = jnp.float32
    f1, s1, g1, t = pl.pallas_call(
        first_kernel,
        out_shape=(
            jax.ShapeDtypeStruct((FIELDS * F0, COLS0), f32),
            jax.ShapeDtypeStruct((FIELDS * F1, COLS0 // 2), f32),
            jax.ShapeDtypeStruct((FIELDS * F1, COLS0 // 2), f32),
            jax.ShapeDtypeStruct((FIELDS * CHUNK, COLS0 // 4), f32),
        ),
        in_specs=[smem(), vmem(), vmem(), vmem()],
        out_specs=(vmem(), vmem(), vmem(), vmem()),
        scratch_shapes=[
            pltpu.VMEM((COLS0 // 128, FIELDS * F0, 128), f32),
            pltpu.VMEM((COLS0 // 256, FIELDS * F1, 128), f32),
        ],
        compiler_params=PARAMS,
    )(band, lo_q, states, hi_q)
    tm2 = shifted(t, "band", 2)
    tm1 = shifted(t, "band", 1)
    tp1 = shifted(t, "band", -1)
    tp2 = shifted(t, "band", -2)
    args = (band, lo_q, states, hi_q, f1, s1, g1, tm2, tm1, t, tp1, tp2)
    last = forecast_slots(SLOTS - 1, 1, args)
    below = shifted(last, "particle", 1)
    picked = forecast_slots(0, SLOTS - 1, args, (local_index, last))
    strip = pl.BlockSpec((1, 2, ROWS0, COLS0), lambda i: (0, 0, 0, 0))
    return pl.pallas_call(
        fix_kernel,
        out_shape=jax.ShapeDtypeStruct(states.shape, f32),
        grid=(1,),
        in_specs=[smem(), strip, strip],
        out_specs=strip,
        input_output_aliases={2: 0},
    )(local_index, below, picked)


def forecast_slots(first, slots, args, pick=None):
    fields = 2 * slots
    block = first // slots

    def rows(count, width):
        return pl.BlockSpec((count, width), lambda i: (block, 0))

    strips = pl.BlockSpec((slots, 2, ROWS0, COLS0), lambda i: (block, 0, 0, 0))
    halos = rows(fields * HALO, COLS0)
    in_specs = [smem(), halos, strips, halos,
                rows(fields * F0, COLS0), rows(fields * F1, COLS0 // 2), rows(fields * F1, COLS0 // 2)]
    in_specs += [rows(fields * CHUNK, COLS0 // 4)] * 5
    f32 = jnp.float32
    out_shape = jax.ShapeDtypeStruct((slots, 2, ROWS0, COLS0), f32)
    out_spec = pl.BlockSpec((slots, 2, ROWS0, COLS0), lambda i: (0, 0, 0, 0))
    extra_scratch = []
    if pick is not None:
        whole = pl.BlockSpec((SLOTS, 2, ROWS0, COLS0), lambda i: (0, 0, 0, 0))
        in_specs = [smem()] + in_specs + [pl.BlockSpec((1, 2, ROWS0, COLS0), lambda i: (0, 0, 0, 0))]
        args = (pick[0],) + tuple(args) + (pick[1],)
        out_shape = jax.ShapeDtypeStruct((SLOTS, 2, ROWS0, COLS0), f32)
        out_spec = whole
        extra_scratch = [pltpu.VMEM((slots, 2, ROWS0, COLS0), f32)]
    work = fields * F0 * COLS0 * 160
    return pl.pallas_call(
        functools.partial(second_kernel, slots, pick is not None),
        out_shape=out_shape,
        grid=(1,),
        in_specs=in_specs,
        out_specs=out_spec,
        scratch_shapes=[
            pltpu.VMEM((fields * F2, COLS0 // 4), f32),
            pltpu.VMEM((fields * F2, COLS0 // 4), f32),
            pltpu.VMEM((COLS0 // 256, 2 * fields * F2, 128), f32),
            pltpu.VMEM((fields * F1, COLS0 // 2), f32),
            pltpu.VMEM((COLS0 // 128, fields * F0, 128), f32),
        ] + extra_scratch,
        compiler_params=PARAMS,
        cost_estimate=pl.CostEstimate(flops=work, transcendentals=0, bytes_accessed=fields * F0 * COLS0 * 16),
    )(*args)


def solution(mesh):
    in_specs = (P("particle", None, "band", None), P())
    out_specs = P("particle", None, "band", None)
    return jax.shard_map(
        per_device, mesh=mesh, in_specs=in_specs, out_specs=out_specs, check_vma=False
    )
```

```python
import functools

import numpy as np
import jax
import jax.numpy as jnp
from jax import lax
from jax.experimental import pallas as pl
from jax.experimental.pallas import tpu as pltpu
from jax.sharding import PartitionSpec as P

GRID_HIERARCHY = 3
COARSE_SWEEPS = 6


smoothing_weight = 0.8
deform_term = 0.1
beta_slope = 0.5
bottom_friction_coefficient = 0.2
time_step = 0.5
meridional_weight = 1.8
zonal_weight = 0.2

SLOTS = 4
FIELDS = 2 * SLOTS
ROWS0 = 16
COLS0 = 1024
F0 = 3 * ROWS0
F1 = F0 // 2
F2 = F1
CHUNK = 8


def diag(level, mode):
    extra = np.float32(deform_term) * np.float32(4.0**level) if mode else np.float32(0.0)
    return float(np.float32(4.0) + extra)


def shifted(value, axis, steps):
    count = lax.axis_size(axis)
    first, last = (max(0, -steps), min(count, count - steps))
    return lax.ppermute(value, axis, [(source, source + steps) for source in range(first, last)])


def rolled(x, shift, axis):
    return pltpu.roll(x, shift % x.shape[axis], axis)


def stencil(f):
    up = rolled(f, -1, 0)
    down = rolled(f, 1, 0)
    along = rolled(f, -1, 1) + rolled(f, 1, 1)
    return meridional_weight * (up + down) + zonal_weight * along


def smooth(f, s, d, mask):
    applied = d * f - stencil(f)
    out = f + smoothing_weight * (s - applied) / d
    return jnp.where(mask, out, 0.0)


def residual(f, s, d, mask):
    return jnp.where(mask, s - (d * f - stencil(f)), 0.0)


def row_mask(band, count, lo, per_device, total):
    rows = band * per_device + lo + lax.broadcasted_iota(jnp.int32, (count, 1), 0)
    return (rows >= 0) & (rows < total)


def pair_matrix(fine, coarse_first):
    if coarse_first:
        shape, fine_dim = (fine // 2, fine), 1
    else:
        shape, fine_dim = (fine, fine // 2), 0
    f_idx = lax.broadcasted_iota(jnp.int32, shape, fine_dim)
    c_idx = lax.broadcasted_iota(jnp.int32, shape, 1 - fine_dim)
    return jnp.where(jnp.right_shift(f_idx, 1) == c_idx, 1.0, 0.0).astype(jnp.bfloat16)


def split_dot(x, m):
    hi = x.astype(jnp.bfloat16)
    rest = x - hi.astype(jnp.float32)
    mid = rest.astype(jnp.bfloat16)
    lo = (rest - mid.astype(jnp.float32)).astype(jnp.bfloat16)
    out = jnp.dot(hi, m, preferred_element_type=jnp.float32)
    out = out + jnp.dot(mid, m, preferred_element_type=jnp.float32)
    return out + jnp.dot(lo, m, preferred_element_type=jnp.float32)


def put_blocks(ref, rows, value):
    for j in range(ref.shape[0]):
        ref[j, rows, :] = value[:, j * 128 : (j + 1) * 128]


def get_blocks(ref, rows):
    return jnp.concatenate([ref[j, rows, :] for j in range(ref.shape[0])], axis=1)


def sources(lo_ref, own_ref, hi_ref, slot):
    q = [
        jnp.concatenate([lo_ref[slot, layer], own_ref[slot, layer], hi_ref[slot, layer]], axis=0)
        for layer in range(2)
    ]
    return q, [-(0.5 * (q[0] + q[1])), -(0.5 * (q[0] - q[1]))]


def first_kernel(band_ref, lo_ref, own_ref, hi_ref, f1_ref, s1_ref, g1_ref, t_ref, r0_ref, r1_ref):
    band = band_ref[0]
    mask0 = row_mask(band, F0, -ROWS0, ROWS0, ROWS0 * 16)
    for slot in range(SLOTS):
        _, src = sources(lo_ref, own_ref, hi_ref, slot)
        for mode in range(2):
            d = diag(0, mode)
            s = src[mode]
            f0 = smoothing_weight * s / d
            f1 = smooth(f0, s, d, mask0)
            rows = pl.ds((2 * slot + mode) * F0, F0)
            f1_ref[rows, :] = f1
            put_blocks(r0_ref, rows, residual(f1, s, d, mask0))
    half = FIELDS * F1
    paired = get_blocks(r0_ref, pl.ds(0, half, stride=2)) + get_blocks(r0_ref, pl.ds(1, half, stride=2))
    s1_ref[...] = split_dot(paired, pair_matrix(COLS0, False))
    mask1 = row_mask(band, F1, -ROWS0 // 2, ROWS0 // 2, ROWS0 * 8)
    for field in range(FIELDS):
        d = diag(1, field % 2)
        rows = pl.ds(field * F1, F1)
        s = s1_ref[rows, :]
        g0 = smoothing_weight * s / d
        g1 = smooth(g0, s, d, mask1)
        g1_ref[rows, :] = g1
        put_blocks(r1_ref, rows, residual(g1, s, d, mask1))
    chunks = []
    for field in range(FIELDS):
        start = field * F1 + ROWS0 // 2
        chunks.append(
            get_blocks(r1_ref, pl.ds(start, CHUNK, stride=2))
            + get_blocks(r1_ref, pl.ds(start + 1, CHUNK, stride=2))
        )
    paired = jnp.concatenate(chunks, axis=0)
    keep = jnp.bitwise_and(lax.broadcasted_iota(jnp.int32, (FIELDS * CHUNK, 1), 0), CHUNK - 1) < ROWS0 // 4
    paired = jnp.where(keep, paired, 0.0)
    t_ref[...] = split_dot(paired, pair_matrix(COLS0 // 2, False))


def second_kernel(
    slots, picks, *refs):
    if picks:
        (index_ref, band_ref, lo_ref, own_ref, hi_ref, f1_ref, s1_ref, g1_ref,
         tm2_ref, tm1_ref, t0_ref, tp1_ref, tp2_ref, last_ref,
         out_ref, s2_ref, e2_ref, up1_ref, g4_ref, up0_ref, own_out) = refs
    else:
        (band_ref, lo_ref, own_ref, hi_ref, f1_ref, s1_ref, g1_ref,
         tm2_ref, tm1_ref, t0_ref, tp1_ref, tp2_ref,
         out_ref, s2_ref, e2_ref, up1_ref, g4_ref, up0_ref) = refs
        own_out = out_ref
    fields = 2 * slots
    band = band_ref[0]
    below = rolled(tm1_ref[...], CHUNK // 2, 0)
    above = rolled(tp1_ref[...], CHUNK // 2, 0)
    for field in range(fields):
        piece = pl.ds(field * CHUNK, CHUNK)
        base = field * F2
        s2_ref[pl.ds(base, CHUNK), :] = tm2_ref[piece, :] + below[field * CHUNK : (field + 1) * CHUNK]
        s2_ref[pl.ds(base + CHUNK, CHUNK), :] = t0_ref[piece, :] + above[field * CHUNK : (field + 1) * CHUNK]
        s2_ref[pl.ds(base + 2 * CHUNK, CHUNK), :] = tp2_ref[piece, :]
    mask2 = row_mask(band, F2, -CHUNK, ROWS0 // 4, ROWS0 * 4)
    for field in range(fields):
        d = diag(2, field % 2)
        rows = pl.ds(field * F2, F2)
        s = s2_ref[rows, :]
        e = smoothing_weight * s / d
        for repeat in range(COARSE_SWEEPS - 1):
            e = smooth(e, s, d, mask2)
        e2_ref[rows, :] = e
    cols = split_dot(e2_ref[...], pair_matrix(COLS0 // 2, True))
    n2 = fields * F2
    put_blocks(up1_ref, pl.ds(0, n2, stride=2), cols)
    put_blocks(up1_ref, pl.ds(1, n2, stride=2), cols)
    mask1 = row_mask(band, F1, -ROWS0 // 2, ROWS0 // 2, ROWS0 * 8)
    for field in range(fields):
        d = diag(1, field % 2)
        rows = pl.ds(field * F1, F1)
        s = s1_ref[rows, :]
        g2 = g1_ref[rows, :] + get_blocks(up1_ref, pl.ds(field * 2 * F2 + CHUNK, F1))
        g3 = smooth(g2, s, d, mask1)
        g4_ref[rows, :] = smooth(g3, s, d, mask1)
    cols = split_dot(g4_ref[...], pair_matrix(COLS0, True))
    n1 = fields * F1
    put_blocks(up0_ref, pl.ds(0, n1, stride=2), cols)
    put_blocks(up0_ref, pl.ds(1, n1, stride=2), cols)
    mask0 = row_mask(band, F0, -ROWS0, ROWS0, ROWS0 * 16)
    for slot in range(slots):
        q, src = sources(lo_ref, own_ref, hi_ref, slot)
        modes = []
        for mode in range(2):
            d = diag(0, mode)
            rows = pl.ds((2 * slot + mode) * F0, F0)
            f2 = f1_ref[rows, :] + get_blocks(up0_ref, rows)
            f3 = smooth(f2, src[mode], d, mask0)
            modes.append(smooth(f3, src[mode], d, mask0))
        streams = [modes[0] + modes[1], modes[0] - modes[1]]
        for layer in range(2):
            stream = streams[layer]
            pv = q[layer]
            stream_x = 0.5 * (rolled(stream, -1, 1) - rolled(stream, 1, 1))
            stream_y = 0.5 * (rolled(stream, -1, 0) - rolled(stream, 1, 0))
            vort_x = 0.5 * (rolled(pv, -1, 1) - rolled(pv, 1, 1))
            vort_y = 0.5 * (rolled(pv, -1, 0) - rolled(pv, 1, 0))
            laplace = stencil(stream) - 4.0 * stream
            drag = bottom_friction_coefficient if layer else 0.0
            jacobian = stream_x * vort_y - stream_y * vort_x
            new = pv - time_step * (jacobian + beta_slope * stream_x + drag * laplace)
            own_out[slot, layer] = new[ROWS0 : 2 * ROWS0]
    if picks:
        pick_slots(index_ref, own_out, last_ref, out_ref)


def pick_slots(index_ref, rest_ref, last_ref, out_ref):
    for slot in range(SLOTS):
        index = index_ref[slot]
        value = last_ref[0]
        for k in range(SLOTS - 2, -1, -1):
            value = jnp.where(index == k + 1, rest_ref[k], value)
        out_ref[slot] = value


def fix_kernel(index_ref, below_ref, current_ref, out_ref, sem):
    del current_ref

    @pl.when(index_ref[0] <= 0)
    def _():
        copy = pltpu.make_async_copy(below_ref.at[0], out_ref.at[0], sem)
        copy.start()
        copy.wait()


def vmem():
    return pl.BlockSpec(memory_space=pltpu.VMEM)


def smem():
    return pl.BlockSpec(memory_space=pltpu.SMEM)


PARAMS = pltpu.CompilerParams(vmem_limit_bytes=48 * 1024 * 1024)


def per_device(states, counts):
    group = lax.axis_index("particle")
    per_group = states.shape[0]
    totals = jnp.cumsum(counts, dtype=jnp.int32)
    slots = group * per_group + jnp.arange(per_group, dtype=jnp.int32)
    ancestor = jnp.sum(
        (totals[None, :] <= slots[:, None]).astype(jnp.int32), axis=1, dtype=jnp.int32
    )
    local_index = ancestor - (group * per_group - 1)

    band = lax.axis_index("band").astype(jnp.int32).reshape(1)
    lo_q = shifted(states, "band", 1)
    hi_q = shifted(states, "band", -1)
    f32 = jnp.float32
    f1, s1, g1, t = pl.pallas_call(
        first_kernel,
        out_shape=(
            jax.ShapeDtypeStruct((FIELDS * F0, COLS0), f32),
            jax.ShapeDtypeStruct((FIELDS * F1, COLS0 // 2), f32),
            jax.ShapeDtypeStruct((FIELDS * F1, COLS0 // 2), f32),
            jax.ShapeDtypeStruct((FIELDS * CHUNK, COLS0 // 4), f32),
        ),
        in_specs=[smem(), vmem(), vmem(), vmem()],
        out_specs=(vmem(), vmem(), vmem(), vmem()),
        scratch_shapes=[
            pltpu.VMEM((COLS0 // 128, FIELDS * F0, 128), f32),
            pltpu.VMEM((COLS0 // 256, FIELDS * F1, 128), f32),
        ],
        compiler_params=PARAMS,
    )(band, lo_q, states, hi_q)
    tm2 = shifted(t, "band", 2)
    tm1 = shifted(t, "band", 1)
    tp1 = shifted(t, "band", -1)
    tp2 = shifted(t, "band", -2)
    args = (band, lo_q, states, hi_q, f1, s1, g1, tm2, tm1, t, tp1, tp2)
    last = forecast_slots(SLOTS - 1, 1, args)
    below = shifted(last, "particle", 1)
    picked = forecast_slots(0, SLOTS - 1, args, (local_index, last))
    anywhere = pl.BlockSpec(memory_space=pl.ANY)
    return pl.pallas_call(
        fix_kernel,
        out_shape=jax.ShapeDtypeStruct(states.shape, f32),
        in_specs=[smem(), vmem(), anywhere],
        out_specs=anywhere,
        scratch_shapes=[pltpu.SemaphoreType.DMA(())],
        input_output_aliases={2: 0},
    )(local_index, below, picked)


def forecast_slots(first, slots, args, pick=None):
    fields = 2 * slots
    block = first // slots

    def rows(count, width):
        return pl.BlockSpec((count, width), lambda i: (block, 0))

    strips = pl.BlockSpec((slots, 2, ROWS0, COLS0), lambda i: (block, 0, 0, 0))
    in_specs = [smem(), strips, strips, strips,
                rows(fields * F0, COLS0), rows(fields * F1, COLS0 // 2), rows(fields * F1, COLS0 // 2)]
    in_specs += [rows(fields * CHUNK, COLS0 // 4)] * 5
    f32 = jnp.float32
    out_shape = jax.ShapeDtypeStruct((slots, 2, ROWS0, COLS0), f32)
    out_spec = pl.BlockSpec((slots, 2, ROWS0, COLS0), lambda i: (0, 0, 0, 0))
    extra_scratch = []
    if pick is not None:
        whole = pl.BlockSpec((SLOTS, 2, ROWS0, COLS0), lambda i: (0, 0, 0, 0))
        in_specs = [smem()] + in_specs + [pl.BlockSpec((1, 2, ROWS0, COLS0), lambda i: (0, 0, 0, 0))]
        args = (pick[0],) + tuple(args) + (pick[1],)
        out_shape = jax.ShapeDtypeStruct((SLOTS, 2, ROWS0, COLS0), f32)
        out_spec = whole
        extra_scratch = [pltpu.VMEM((slots, 2, ROWS0, COLS0), f32)]
    work = fields * F0 * COLS0 * 160
    return pl.pallas_call(
        functools.partial(second_kernel, slots, pick is not None),
        out_shape=out_shape,
        grid=(1,),
        in_specs=in_specs,
        out_specs=out_spec,
        scratch_shapes=[
            pltpu.VMEM((fields * F2, COLS0 // 4), f32),
            pltpu.VMEM((fields * F2, COLS0 // 4), f32),
            pltpu.VMEM((COLS0 // 256, 2 * fields * F2, 128), f32),
            pltpu.VMEM((fields * F1, COLS0 // 2), f32),
            pltpu.VMEM((COLS0 // 128, fields * F0, 128), f32),
        ] + extra_scratch,
        compiler_params=PARAMS,
        cost_estimate=pl.CostEstimate(flops=work, transcendentals=0, bytes_accessed=fields * F0 * COLS0 * 16),
    )(*args)


def solution(mesh):
    in_specs = (P("particle", None, "band", None), P())
    out_specs = P("particle", None, "band", None)
    return jax.shard_map(
        per_device, mesh=mesh, in_specs=in_specs, out_specs=out_specs, check_vma=False
    )
```

```python
import functools

import numpy as np
import jax
import jax.numpy as jnp
from jax import lax
from jax.experimental import pallas as pl
from jax.experimental.pallas import tpu as pltpu
from jax.sharding import PartitionSpec as P

GRID_HIERARCHY = 3
COARSE_SWEEPS = 6


smoothing_weight = 0.8
deform_term = 0.1
beta_slope = 0.5
bottom_friction_coefficient = 0.2
time_step = 0.5
meridional_weight = 1.8
zonal_weight = 0.2

SLOTS = 4
FIELDS = 2 * SLOTS
ROWS0 = 16
COLS0 = 1024
F0 = 3 * ROWS0
F1 = F0 // 2
F2 = F1
CHUNK = 8


def diag(level, mode):
    extra = np.float32(deform_term) * np.float32(4.0**level) if mode else np.float32(0.0)
    return float(np.float32(4.0) + extra)


def shifted(value, axis, steps):
    count = lax.axis_size(axis)
    first, last = (max(0, -steps), min(count, count - steps))
    return lax.ppermute(value, axis, [(source, source + steps) for source in range(first, last)])


def rolled(x, shift, axis):
    return pltpu.roll(x, shift % x.shape[axis], axis)


def stencil(f):
    up = rolled(f, -1, 0)
    down = rolled(f, 1, 0)
    along = rolled(f, -1, 1) + rolled(f, 1, 1)
    return meridional_weight * (up + down) + zonal_weight * along


def smooth(f, s, d, mask):
    applied = d * f - stencil(f)
    out = f + smoothing_weight * (s - applied) / d
    return jnp.where(mask, out, 0.0)


def residual(f, s, d, mask):
    return jnp.where(mask, s - (d * f - stencil(f)), 0.0)


def row_mask(band, count, lo, per_device, total):
    rows = band * per_device + lo + lax.broadcasted_iota(jnp.int32, (count, 1), 0)
    return (rows >= 0) & (rows < total)


def pair_matrix(fine, coarse_first):
    if coarse_first:
        shape, fine_dim = (fine // 2, fine), 1
    else:
        shape, fine_dim = (fine, fine // 2), 0
    f_idx = lax.broadcasted_iota(jnp.int32, shape, fine_dim)
    c_idx = lax.broadcasted_iota(jnp.int32, shape, 1 - fine_dim)
    return jnp.where(jnp.right_shift(f_idx, 1) == c_idx, 1.0, 0.0).astype(jnp.bfloat16)


def split_dot(x, m):
    hi = x.astype(jnp.bfloat16)
    rest = x - hi.astype(jnp.float32)
    mid = rest.astype(jnp.bfloat16)
    lo = (rest - mid.astype(jnp.float32)).astype(jnp.bfloat16)
    out = jnp.dot(hi, m, preferred_element_type=jnp.float32)
    out = out + jnp.dot(mid, m, preferred_element_type=jnp.float32)
    return out + jnp.dot(lo, m, preferred_element_type=jnp.float32)


def put_blocks(ref, rows, value):
    for j in range(ref.shape[0]):
        ref[j, rows, :] = value[:, j * 128 : (j + 1) * 128]


def get_blocks(ref, rows):
    return jnp.concatenate([ref[j, rows, :] for j in range(ref.shape[0])], axis=1)


def sources(lo_ref, own_ref, hi_ref, slot):
    q = [
        jnp.concatenate([lo_ref[slot, layer], own_ref[slot, layer], hi_ref[slot, layer]], axis=0)
        for layer in range(2)
    ]
    return q, [-(0.5 * (q[0] + q[1])), -(0.5 * (q[0] - q[1]))]


def first_kernel(band_ref, lo_ref, own_ref, hi_ref, f1_ref, s1_ref, g1_ref, t_ref, r0_ref, r1_ref):
    band = band_ref[0]
    mask0 = row_mask(band, F0, -ROWS0, ROWS0, ROWS0 * 16)
    for slot in range(SLOTS):
        _, src = sources(lo_ref, own_ref, hi_ref, slot)
        for mode in range(2):
            d = diag(0, mode)
            s = src[mode]
            f0 = smoothing_weight * s / d
            f1 = smooth(f0, s, d, mask0)
            rows = pl.ds((2 * slot + mode) * F0, F0)
            if slot == SLOTS - 1:
                f1_ref[pl.ds(mode * F0, F0), :] = f1
            put_blocks(r0_ref, rows, residual(f1, s, d, mask0))
    half = FIELDS * F1
    paired = get_blocks(r0_ref, pl.ds(0, half, stride=2)) + get_blocks(r0_ref, pl.ds(1, half, stride=2))
    s1_ref[...] = split_dot(paired, pair_matrix(COLS0, False))
    mask1 = row_mask(band, F1, -ROWS0 // 2, ROWS0 // 2, ROWS0 * 8)
    for field in range(FIELDS):
        d = diag(1, field % 2)
        rows = pl.ds(field * F1, F1)
        s = s1_ref[rows, :]
        g0 = smoothing_weight * s / d
        g1 = smooth(g0, s, d, mask1)
        g1_ref[rows, :] = g1
        put_blocks(r1_ref, rows, residual(g1, s, d, mask1))
    chunks = []
    for field in range(FIELDS):
        start = field * F1 + ROWS0 // 2
        chunks.append(
            get_blocks(r1_ref, pl.ds(start, CHUNK, stride=2))
            + get_blocks(r1_ref, pl.ds(start + 1, CHUNK, stride=2))
        )
    paired = jnp.concatenate(chunks, axis=0)
    keep = jnp.bitwise_and(lax.broadcasted_iota(jnp.int32, (FIELDS * CHUNK, 1), 0), CHUNK - 1) < ROWS0 // 4
    paired = jnp.where(keep, paired, 0.0)
    t_ref[...] = split_dot(paired, pair_matrix(COLS0 // 2, False))


def second_kernel(
    slots, picks, *refs):
    if picks:
        (index_ref, band_ref, lo_ref, own_ref, hi_ref, f1_ref, s1_ref, g1_ref,
         tm2_ref, tm1_ref, t0_ref, tp1_ref, tp2_ref, last_ref,
         out_ref, s2_ref, e2_ref, up1_ref, g4_ref, up0_ref, own_out) = refs
    else:
        (band_ref, lo_ref, own_ref, hi_ref, f1_ref, s1_ref, g1_ref,
         tm2_ref, tm1_ref, t0_ref, tp1_ref, tp2_ref,
         out_ref, s2_ref, e2_ref, up1_ref, g4_ref, up0_ref) = refs
        own_out = out_ref
    fields = 2 * slots
    band = band_ref[0]
    below = rolled(tm1_ref[...], CHUNK // 2, 0)
    above = rolled(tp1_ref[...], CHUNK // 2, 0)
    for field in range(fields):
        piece = pl.ds(field * CHUNK, CHUNK)
        base = field * F2
        s2_ref[pl.ds(base, CHUNK), :] = tm2_ref[piece, :] + below[field * CHUNK : (field + 1) * CHUNK]
        s2_ref[pl.ds(base + CHUNK, CHUNK), :] = t0_ref[piece, :] + above[field * CHUNK : (field + 1) * CHUNK]
        s2_ref[pl.ds(base + 2 * CHUNK, CHUNK), :] = tp2_ref[piece, :]
    mask2 = row_mask(band, F2, -CHUNK, ROWS0 // 4, ROWS0 * 4)
    for field in range(fields):
        d = diag(2, field % 2)
        rows = pl.ds(field * F2, F2)
        s = s2_ref[rows, :]
        e = smoothing_weight * s / d
        for repeat in range(COARSE_SWEEPS - 1):
            e = smooth(e, s, d, mask2)
        e2_ref[rows, :] = e
    cols = split_dot(e2_ref[...], pair_matrix(COLS0 // 2, True))
    n2 = fields * F2
    put_blocks(up1_ref, pl.ds(0, n2, stride=2), cols)
    put_blocks(up1_ref, pl.ds(1, n2, stride=2), cols)
    mask1 = row_mask(band, F1, -ROWS0 // 2, ROWS0 // 2, ROWS0 * 8)
    for field in range(fields):
        d = diag(1, field % 2)
        rows = pl.ds(field * F1, F1)
        s = s1_ref[rows, :]
        g2 = g1_ref[rows, :] + get_blocks(up1_ref, pl.ds(field * 2 * F2 + CHUNK, F1))
        g3 = smooth(g2, s, d, mask1)
        g4_ref[rows, :] = smooth(g3, s, d, mask1)
    cols = split_dot(g4_ref[...], pair_matrix(COLS0, True))
    n1 = fields * F1
    put_blocks(up0_ref, pl.ds(0, n1, stride=2), cols)
    put_blocks(up0_ref, pl.ds(1, n1, stride=2), cols)
    mask0 = row_mask(band, F0, -ROWS0, ROWS0, ROWS0 * 16)
    for slot in range(slots):
        q, src = sources(lo_ref, own_ref, hi_ref, slot)
        modes = []
        for mode in range(2):
            d = diag(0, mode)
            rows = pl.ds((2 * slot + mode) * F0, F0)
            if picks:
                f1 = smooth(smoothing_weight * src[mode] / d, src[mode], d, mask0)
            else:
                f1 = f1_ref[pl.ds(mode * F0, F0), :]
            f2 = f1 + get_blocks(up0_ref, rows)
            f3 = smooth(f2, src[mode], d, mask0)
            modes.append(smooth(f3, src[mode], d, mask0))
        streams = [modes[0] + modes[1], modes[0] - modes[1]]
        for layer in range(2):
            stream = streams[layer]
            pv = q[layer]
            stream_x = 0.5 * (rolled(stream, -1, 1) - rolled(stream, 1, 1))
            stream_y = 0.5 * (rolled(stream, -1, 0) - rolled(stream, 1, 0))
            vort_x = 0.5 * (rolled(pv, -1, 1) - rolled(pv, 1, 1))
            vort_y = 0.5 * (rolled(pv, -1, 0) - rolled(pv, 1, 0))
            laplace = stencil(stream) - 4.0 * stream
            drag = bottom_friction_coefficient if layer else 0.0
            jacobian = stream_x * vort_y - stream_y * vort_x
            new = pv - time_step * (jacobian + beta_slope * stream_x + drag * laplace)
            own_out[slot, layer] = new[ROWS0 : 2 * ROWS0]
    if picks:
        pick_slots(index_ref, own_out, last_ref, out_ref)


def pick_slots(index_ref, rest_ref, last_ref, out_ref):
    for slot in range(SLOTS):
        index = index_ref[slot]
        value = last_ref[0]
        for k in range(SLOTS - 2, -1, -1):
            value = jnp.where(index == k + 1, rest_ref[k], value)
        out_ref[slot] = value


def fix_kernel(index_ref, below_ref, current_ref, out_ref):
    out_ref[0] = jnp.where(index_ref[0] <= 0, below_ref[0], current_ref[0])


def vmem():
    return pl.BlockSpec(memory_space=pltpu.VMEM)


def smem():
    return pl.BlockSpec(memory_space=pltpu.SMEM)


PARAMS = pltpu.CompilerParams(vmem_limit_bytes=48 * 1024 * 1024)


def per_device(states, counts):
    group = lax.axis_index("particle")
    per_group = states.shape[0]
    totals = jnp.cumsum(counts, dtype=jnp.int32)
    slots = group * per_group + jnp.arange(per_group, dtype=jnp.int32)
    ancestor = jnp.sum(
        (totals[None, :] <= slots[:, None]).astype(jnp.int32), axis=1, dtype=jnp.int32
    )
    local_index = ancestor - (group * per_group - 1)

    band = lax.axis_index("band").astype(jnp.int32).reshape(1)
    lo_q = shifted(states, "band", 1)
    hi_q = shifted(states, "band", -1)
    f32 = jnp.float32
    f1, s1, g1, t = pl.pallas_call(
        first_kernel,
        out_shape=(
            jax.ShapeDtypeStruct((2 * F0, COLS0), f32),
            jax.ShapeDtypeStruct((FIELDS * F1, COLS0 // 2), f32),
            jax.ShapeDtypeStruct((FIELDS * F1, COLS0 // 2), f32),
            jax.ShapeDtypeStruct((FIELDS * CHUNK, COLS0 // 4), f32),
        ),
        in_specs=[smem(), vmem(), vmem(), vmem()],
        out_specs=(vmem(), vmem(), vmem(), vmem()),
        scratch_shapes=[
            pltpu.VMEM((COLS0 // 128, FIELDS * F0, 128), f32),
            pltpu.VMEM((COLS0 // 256, FIELDS * F1, 128), f32),
        ],
        compiler_params=PARAMS,
    )(band, lo_q, states, hi_q)
    tm2 = shifted(t, "band", 2)
    tm1 = shifted(t, "band", 1)
    tp1 = shifted(t, "band", -1)
    tp2 = shifted(t, "band", -2)
    args = (band, lo_q, states, hi_q, f1, s1, g1, tm2, tm1, t, tp1, tp2)
    last = forecast_slots(SLOTS - 1, 1, args)
    below = shifted(last, "particle", 1)
    picked = forecast_slots(0, SLOTS - 1, args, (local_index, last))
    strip = pl.BlockSpec((1, 2, ROWS0, COLS0), lambda i: (0, 0, 0, 0))
    return pl.pallas_call(
        fix_kernel,
        out_shape=jax.ShapeDtypeStruct(states.shape, f32),
        grid=(1,),
        in_specs=[smem(), strip, strip],
        out_specs=strip,
        input_output_aliases={2: 0},
    )(local_index, below, picked)


def forecast_slots(first, slots, args, pick=None):
    fields = 2 * slots
    block = first // slots

    def rows(count, width):
        return pl.BlockSpec((count, width), lambda i: (block, 0))

    strips = pl.BlockSpec((slots, 2, ROWS0, COLS0), lambda i: (block, 0, 0, 0))
    in_specs = [smem(), strips, strips, strips,
                pl.BlockSpec((2 * F0, COLS0), lambda i: (0, 0)), rows(fields * F1, COLS0 // 2), rows(fields * F1, COLS0 // 2)]
    in_specs += [rows(fields * CHUNK, COLS0 // 4)] * 5
    f32 = jnp.float32
    out_shape = jax.ShapeDtypeStruct((slots, 2, ROWS0, COLS0), f32)
    out_spec = pl.BlockSpec((slots, 2, ROWS0, COLS0), lambda i: (0, 0, 0, 0))
    extra_scratch = []
    if pick is not None:
        whole = pl.BlockSpec((SLOTS, 2, ROWS0, COLS0), lambda i: (0, 0, 0, 0))
        in_specs = [smem()] + in_specs + [pl.BlockSpec((1, 2, ROWS0, COLS0), lambda i: (0, 0, 0, 0))]
        args = (pick[0],) + tuple(args) + (pick[1],)
        out_shape = jax.ShapeDtypeStruct((SLOTS, 2, ROWS0, COLS0), f32)
        out_spec = whole
        extra_scratch = [pltpu.VMEM((slots, 2, ROWS0, COLS0), f32)]
    work = fields * F0 * COLS0 * 160
    return pl.pallas_call(
        functools.partial(second_kernel, slots, pick is not None),
        out_shape=out_shape,
        grid=(1,),
        in_specs=in_specs,
        out_specs=out_spec,
        scratch_shapes=[
            pltpu.VMEM((fields * F2, COLS0 // 4), f32),
            pltpu.VMEM((fields * F2, COLS0 // 4), f32),
            pltpu.VMEM((COLS0 // 256, 2 * fields * F2, 128), f32),
            pltpu.VMEM((fields * F1, COLS0 // 2), f32),
            pltpu.VMEM((COLS0 // 128, fields * F0, 128), f32),
        ] + extra_scratch,
        compiler_params=PARAMS,
        cost_estimate=pl.CostEstimate(flops=work, transcendentals=0, bytes_accessed=fields * F0 * COLS0 * 16),
    )(*args)


def solution(mesh):
    in_specs = (P("particle", None, "band", None), P())
    out_specs = P("particle", None, "band", None)
    return jax.shard_map(
        per_device, mesh=mesh, in_specs=in_specs, out_specs=out_specs, check_vma=False
    )
```
